128 devices in a mesh: row: 8 (over x, core), col: 16 (over y, z).
Axes of the slice: x: 4, y: 4, z: 4, core: 2. Of those that a mesh axis runs over, the one named last changes fastest.
Arguments:
- front_matrix: float32 [16384, 16384], P('row', 'col'), may hold values from -2.5 to 202.5, as said below
- child_schur: float32 [2, 8192, 8192], P(None, 'row', 'col'), may hold values from -1.25 to 1.25
- child_index: int32 [2, 128], replicated, may hold values from 0 to 255, as said below
- child_valid: int32 [2, 128], replicated, may hold values 0 or 1
Outputs:
- trailing: float32 [16384, 16384], P('row', 'col')
- panel_factor: float32 [16384, 512], P('row')
The draws below stay inside these ranges and needn't reach their ends.
Inputs may be any that keep to these rules, and one draw needn't show every extreme that they name: `front_matrix`: off the logical diagonal the entries lie in -2.5 to 2.5, on it in 97.5 to 202.5. `child_index`: each child's 128 entries are distinct front blocks. Among the child blocks a that share a mod 8, exactly 2 land in front blocks of each value mod 8; among the child blocks b that share b mod 16, at most 1 land in front blocks of any one value mod 16, and some value takes exactly 1.
All inputs are finite; a program needn't handle non-finite values.
Results may differ from the reference program's by a relative error of at most 0.00005.
Values sent between devices are 32-bit elements; how exact they have to be, the bound alone decides.
No kernel may reach another device: no remote copies, remote signals or barrier semaphores. Data moves between devices by JAX's collectives and lax.ppermute only.
A program may use at most 256 MiB of HBM per device.

```python
import jax
import jax.numpy as jnp
from jax import lax

FRONT = 16384
CHILD = 8192
PANEL = 512
BLK = 64
NB = 256
CB = 128
RB = 32
KB = 16
CC = 8
N_ROW = 8
N_COL = 16


def draw_front_matrix(key, part):
    row_devices = NB // RB
    col_devices = NB // KB
    base_key, diag_key = jax.random.split(key)
    entries = jax.random.truncated_normal(base_key, -2.5, 2.5, (FRONT, FRONT), jnp.float32)
    positions = jnp.arange(FRONT)
    stored_block = positions // BLK
    logical_row = (stored_block % RB * row_devices + stored_block // RB) * BLK + positions % BLK
    logical_col = (stored_block % KB * col_devices + stored_block // KB) * BLK + positions % BLK
    boost = jax.random.uniform(diag_key, (FRONT,), jnp.float32, 100.0, 200.0)
    return entries + jnp.where(logical_row[:, None] == logical_col[None, :], boost[logical_row][:, None], 0.0)


def draw_child_schur(key, part):
    return 0.5 * jax.random.truncated_normal(key, -2.5, 2.5, (2, CHILD, CHILD), jnp.float32)


def draw_child_index(key, part):
    col_devices = NB // KB
    lists = []
    for child_number in range(2):
        base = jax.random.fold_in(key, 17 + child_number)
        perm_key, shift_key, slot_key = jax.random.split(base, 3)
        orders = jax.vmap(lambda sub_key: jax.random.permutation(sub_key, CC))(jax.random.split(perm_key, col_devices))
        rotation = jax.random.randint(shift_key, (), 0, col_devices)
        all_blocks = jnp.arange(CB)
        column_group = all_blocks % col_devices
        column_step = all_blocks // col_devices
        residue = (column_group + orders[column_group, column_step] + rotation) % col_devices
        earlier = (residue[:, None] == residue[None, :]) & (all_blocks[None, :] < all_blocks[:, None])
        order_rank = jnp.sum(earlier.astype(jnp.int32), axis=1)
        slots = jax.vmap(lambda sub_key: jax.random.permutation(sub_key, KB))(jax.random.split(slot_key, col_devices))
        quotient = slots[residue, order_rank]
        lists.append(quotient * col_devices + residue)
    return jnp.stack(lists).astype(jnp.int32)


def touch_ends(result, rng, least, high):
    longest = result.shape.index(max(result.shape))
    spots = []
    for shift in (0, 1):
        where = [jax.random.randint(jax.random.fold_in(rng, axis), (), 0, length) for axis, length in enumerate(result.shape)]
        where[longest] = (where[longest] + shift) % result.shape[longest]
        spots.append(tuple(where))
    return result.at[spots[0]].set(least).at[spots[1]].set(high)


def setup_inputs(seed: int = 0) -> dict:
    keys = jax.random.split(jax.random.key(seed), 5)
    front_matrix = draw_front_matrix(jax.random.fold_in(keys[4], 71), 0)
    child_schur = draw_child_schur(jax.random.fold_in(keys[4], 71), 0)
    child_index = draw_child_index(jax.random.fold_in(keys[4], 71), 0)
    child_valid = touch_ends((jax.random.randint(keys[3], (2, CB), 0, 4) < 3).astype(jnp.int32), jax.random.fold_in(keys[3], 1), 0, 1)
    return dict(front_matrix=front_matrix, child_schur=child_schur, child_index=child_index, child_valid=child_valid)


def stored_rows(total_blocks, devices):
    per_device = total_blocks // devices
    logical = jnp.arange(total_blocks)
    stored = logical % devices * per_device + logical // devices
    return (stored[:, None] * BLK + jnp.arange(BLK)[None, :]).reshape(-1).astype(jnp.int32)

def reference(front_matrix, child_schur, child_index, child_valid):
    row_perm = stored_rows(NB, N_ROW)
    col_perm = stored_rows(NB, N_COL)
    front_l = front_matrix[row_perm][:, col_perm]
    blocked = front_l.reshape(NB, BLK, NB, BLK).transpose(0, 2, 1, 3)
    child_rows = stored_rows(CB, N_ROW)
    child_cols = stored_rows(CB, N_COL)
    for child_number in range(2):
        child_l = child_schur[child_number][child_rows][:, child_cols]
        pieces = child_l.reshape(CB, BLK, CB, BLK).transpose(0, 2, 1, 3)
        weight = child_valid[child_number].astype(jnp.float32)
        pieces = pieces * (weight[:, None] * weight[None, :])[:, :, None, None]
        target = child_index[child_number].astype(jnp.int32)
        blocked = blocked.at[target[:, None], target[None, :]].add(pieces)
    extended = blocked.transpose(0, 2, 1, 3).reshape(FRONT, FRONT)
    lower_factor = jnp.linalg.cholesky(extended[:PANEL, :PANEL])
    solved = jax.scipy.linalg.solve_triangular(lower_factor, extended[PANEL:, :PANEL].T, lower=True).T
    panel_l = jnp.concatenate([lower_factor, solved], axis=0)
    update = jnp.dot(panel_l.astype(jnp.float32), panel_l.T.astype(jnp.float32), precision=lax.Precision.HIGHEST, preferred_element_type=jnp.float32)
    retained = jnp.arange(FRONT) >= PANEL
    trailing_l = jnp.where(retained[:, None] & retained[None, :], extended - update, jnp.zeros_like(update))
    trailing = jnp.zeros_like(trailing_l).at[row_perm].set(trailing_l)
    trailing = jnp.zeros_like(trailing).at[:, col_perm].set(trailing)
    panel_factor = jnp.zeros((FRONT, PANEL), jnp.float32).at[row_perm].set(panel_l)
    return (trailing, panel_factor)
```

```python
import jax
import jax.numpy as jnp
from jax import lax
from jax.sharding import PartitionSpec as P

CHILD = 8192
PANEL = 512
BLK = 64


exact_mode = lax.Precision.HIGHEST


def take_slabs(source, indices):
    return jnp.take(source, indices, axis=0)


def on_device(front_matrix, child_schur, child_index, child_valid):
    row_count = lax.axis_size("row")
    col_count = lax.axis_size("col")
    row_place = lax.axis_index("row")
    col_place = lax.axis_index("col")
    local_rows, local_cols = front_matrix.shape
    row_blocks = local_rows // BLK
    col_blocks = local_cols // BLK
    child_blocks = CHILD // BLK
    child_rowblk = child_schur.shape[1] // BLK
    child_colblk = child_schur.shape[2] // BLK
    per_owner = child_blocks // (row_count * row_count)
    col_multi = max(1, child_blocks // (col_count * col_count))
    row_slots = row_count * per_owner
    col_slots = col_count * col_multi
    validity = child_valid.astype(jnp.float32)
    all_blocks = jnp.arange(child_blocks)
    owner_row = child_index % row_count
    owner_col = child_index % col_count
    sender_row = all_blocks % row_count
    sender_col = all_blocks % col_count
    before = all_blocks[None, :] < all_blocks[:, None]
    earlier_row = (sender_row[:, None] == sender_row[None, :]) & before
    earlier_col = (sender_col[:, None] == sender_col[None, :]) & before
    row_rank = jnp.sum(
        (earlier_row[None] & (owner_row[:, :, None] == owner_row[:, None, :])).astype(jnp.int32),
        axis=2,
    )
    col_rank = jnp.sum(
        (earlier_col[None] & (owner_col[:, :, None] == owner_col[:, None, :])).astype(jnp.int32),
        axis=2,
    )
    row_key = owner_row * per_owner + row_rank
    col_key = owner_col * col_multi + col_rank
    local_arow = row_place + row_count * jnp.arange(child_rowblk)
    mine_rowkey = jnp.take(row_key, local_arow, axis=1)
    row_hit_send = mine_rowkey[:, :, None] == jnp.arange(row_slots)[None, None, :]
    src_row = jnp.sum(
        row_hit_send.astype(jnp.int32) * jnp.arange(child_rowblk)[None, :, None], axis=1
    )
    local_bcol = col_place + col_count * jnp.arange(child_colblk)
    mine_colkey = jnp.take(col_key, local_bcol, axis=1)
    col_hit_send = mine_colkey[:, :, None] == jnp.arange(col_slots)[None, None, :]
    src_col = jnp.sum(
        col_hit_send.astype(jnp.int32) * jnp.arange(child_colblk)[None, :, None], axis=1
    )
    has_col = jnp.sum(col_hit_send.astype(jnp.float32), axis=1)

    blocks = child_schur.reshape(2, child_rowblk, BLK, child_colblk * BLK)
    outgoing = jax.vmap(take_slabs)(blocks, src_row)
    outgoing = outgoing.reshape(2, row_slots * BLK, child_colblk * BLK)
    section_one = lax.all_to_all(outgoing, "row", split_axis=1, concat_axis=1, tiled=True)
    flipped = jnp.swapaxes(section_one, 1, 2).reshape(2, child_colblk, BLK, row_slots * BLK)
    onward = jax.vmap(take_slabs)(flipped, src_col) * has_col[:, :, None, None]
    onward = onward.reshape(2, col_slots * BLK, row_slots * BLK)
    section_two = lax.all_to_all(onward, "col", split_axis=1, concat_axis=1, tiled=True)
    arrived = section_two.reshape(2, col_slots, BLK, row_slots * BLK)

    front_rowblk = row_place + row_count * jnp.arange(row_blocks)
    match_rows = (child_index[:, None, :] == front_rowblk[None, :, None]).astype(jnp.int32)
    row_slot_of = sender_row[None, :] * per_owner + row_rank
    row_source = jnp.sum(match_rows * row_slot_of[:, None, :], axis=2)
    row_weight = jnp.sum(match_rows.astype(jnp.float32) * validity[:, None, :], axis=2)
    front_colblk = col_place + col_count * jnp.arange(col_blocks)
    match_cols = (child_index[:, None, :] == front_colblk[None, :, None]).astype(jnp.int32)
    col_slot_of = sender_col[None, :] * col_multi + col_rank
    col_source = jnp.sum(match_cols * col_slot_of[:, None, :], axis=2)
    col_weight = jnp.sum(match_cols.astype(jnp.float32) * validity[:, None, :], axis=2)

    by_col = jax.vmap(take_slabs)(arrived, col_source) * col_weight[:, :, None, None]
    by_col = by_col.reshape(2, local_cols, row_slots * BLK)
    unflipped = jnp.swapaxes(by_col, 1, 2).reshape(2, row_slots, BLK, local_cols)
    placed = jax.vmap(take_slabs)(unflipped, row_source) * row_weight[:, :, None, None]
    placed = placed.reshape(2, local_rows, local_cols)
    extended = front_matrix + placed[0] + placed[1]

    panel_width = PANEL // BLK
    spread = col_count // panel_width
    lead = extended[:, :BLK]
    lifted = lax.ppermute(
        lead, "col", [(c, c + panel_width * s) for s in range(1, spread) for c in range(panel_width)]
    )
    mine = jnp.where(col_place < panel_width, lead, lifted)
    part_rows = local_rows // spread
    part = lax.dynamic_slice_in_dim(mine, (col_place // panel_width) * part_rows, part_rows, axis=0)
    gathered = lax.all_gather(part, "col", axis=0, tiled=False)
    gathered = gathered.reshape(spread, panel_width, part_rows, BLK)
    panel_cols = gathered.transpose(0, 2, 1, 3).reshape(local_rows, PANEL)

    corner = lax.all_gather(panel_cols[: PANEL // row_count], "row", axis=0, tiled=True)
    lower_factor = jnp.linalg.cholesky(corner)
    solved = jax.scipy.linalg.solve_triangular(lower_factor, panel_cols.T, lower=True).T
    logical_blk = jnp.arange(row_blocks) * row_count + row_place
    factor_blocks = lower_factor.reshape(panel_width, BLK, PANEL)
    picked = jnp.take(factor_blocks, jnp.minimum(logical_blk, panel_width - 1), axis=0)
    in_panel = (logical_blk < panel_width)[:, None, None]
    panel_factor = jnp.where(in_panel, picked, solved.reshape(row_blocks, BLK, PANEL)).reshape(
        local_rows, PANEL
    )

    ratio = col_count // row_count
    arranged = panel_factor.reshape(col_blocks, ratio, BLK, PANEL)
    chosen = lax.dynamic_index_in_dim(arranged, col_place // row_count, axis=1, keepdims=False)
    chosen = chosen.reshape(col_blocks * BLK, PANEL)
    pairs = []
    for r0 in range(row_count):
        for c1 in range(col_count):
            dest_row = c1 % row_count
            dest_col = r0 + row_count * (c1 // row_count)
            pairs.append((r0 * col_count + c1, dest_row * col_count + dest_col))
    across = lax.ppermute(chosen, ("row", "col"), pairs)
    update = jnp.einsum("rp,cp->rc", panel_factor, across, precision=exact_mode)
    logical_row = jnp.arange(local_rows) // BLK * row_count + row_place
    logical_col = jnp.arange(local_cols) // BLK * col_count + col_place
    retained = (logical_row >= panel_width)[:, None] & (logical_col >= panel_width)[None, :]
    trailing = jnp.where(retained, extended - update, jnp.zeros_like(update))
    return (trailing, panel_factor)


def solution(mesh):
    in_specs = (P("row", "col"), P(None, "row", "col"), P(), P())
    out_specs = (P("row", "col"), P("row", None))
    return jax.shard_map(
        on_device, mesh=mesh, in_specs=in_specs, out_specs=out_specs, check_vma=False
    )
```

```python
import jax
import jax.numpy as jnp
from jax import lax
from jax.sharding import PartitionSpec as P

CHILD = 8192
PANEL = 512
BLK = 64


exact_mode = lax.Precision.HIGHEST


def take_slabs(source, indices):
    return jnp.take(source, indices, axis=0)


def on_device(front_matrix, child_schur, child_index, child_valid):
    row_count = lax.axis_size("row")
    col_count = lax.axis_size("col")
    row_place = lax.axis_index("row")
    col_place = lax.axis_index("col")
    local_rows, local_cols = front_matrix.shape
    row_blocks = local_rows // BLK
    col_blocks = local_cols // BLK
    child_blocks = CHILD // BLK
    child_rowblk = child_schur.shape[1] // BLK
    child_colblk = child_schur.shape[2] // BLK
    per_owner = child_blocks // (row_count * row_count)
    col_multi = max(1, child_blocks // (col_count * col_count))
    row_slots = row_count * per_owner
    col_slots = col_count * col_multi
    validity = child_valid.astype(jnp.float32)
    all_blocks = jnp.arange(child_blocks)
    owner_row = child_index % row_count
    owner_col = child_index % col_count
    sender_row = all_blocks % row_count
    sender_col = all_blocks % col_count
    before = all_blocks[None, :] < all_blocks[:, None]
    earlier_row = (sender_row[:, None] == sender_row[None, :]) & before
    earlier_col = (sender_col[:, None] == sender_col[None, :]) & before
    row_rank = jnp.sum(
        (earlier_row[None] & (owner_row[:, :, None] == owner_row[:, None, :])).astype(jnp.int32),
        axis=2,
    )
    col_rank = jnp.sum(
        (earlier_col[None] & (owner_col[:, :, None] == owner_col[:, None, :])).astype(jnp.int32),
        axis=2,
    )
    row_key = owner_row * per_owner + row_rank
    col_key = owner_col * col_multi + col_rank
    local_arow = row_place + row_count * jnp.arange(child_rowblk)
    mine_rowkey = jnp.take(row_key, local_arow, axis=1)
    row_hit_send = mine_rowkey[:, :, None] == jnp.arange(row_slots)[None, None, :]
    src_row = jnp.sum(
        row_hit_send.astype(jnp.int32) * jnp.arange(child_rowblk)[None, :, None], axis=1
    )
    local_bcol = col_place + col_count * jnp.arange(child_colblk)
    mine_colkey = jnp.take(col_key, local_bcol, axis=1)
    col_hit_send = mine_colkey[:, :, None] == jnp.arange(col_slots)[None, None, :]
    src_col = jnp.sum(
        col_hit_send.astype(jnp.int32) * jnp.arange(child_colblk)[None, :, None], axis=1
    )
    has_col = jnp.sum(col_hit_send.astype(jnp.float32), axis=1)

    blocks = child_schur.reshape(2, child_rowblk, BLK, child_colblk * BLK)
    arrived = []
    for k in range(2):
        outgoing = take_slabs(blocks[k], src_row[k]).reshape(row_slots * BLK, child_colblk * BLK)
        section_one = lax.all_to_all(outgoing, "row", split_axis=0, concat_axis=0, tiled=True)
        flipped = section_one.T.reshape(child_colblk, BLK, row_slots * BLK)
        onward = take_slabs(flipped, src_col[k]) * has_col[k][:, None, None]
        onward = onward.reshape(col_slots * BLK, row_slots * BLK)
        section_two = lax.all_to_all(onward, "col", split_axis=0, concat_axis=0, tiled=True)
        arrived.append(section_two.reshape(col_slots, BLK, row_slots * BLK))
    arrived = jnp.stack(arrived)

    front_rowblk = row_place + row_count * jnp.arange(row_blocks)
    match_rows = (child_index[:, None, :] == front_rowblk[None, :, None]).astype(jnp.int32)
    row_slot_of = sender_row[None, :] * per_owner + row_rank
    row_source = jnp.sum(match_rows * row_slot_of[:, None, :], axis=2)
    row_weight = jnp.sum(match_rows.astype(jnp.float32) * validity[:, None, :], axis=2)
    front_colblk = col_place + col_count * jnp.arange(col_blocks)
    match_cols = (child_index[:, None, :] == front_colblk[None, :, None]).astype(jnp.int32)
    col_slot_of = sender_col[None, :] * col_multi + col_rank
    col_source = jnp.sum(match_cols * col_slot_of[:, None, :], axis=2)
    col_weight = jnp.sum(match_cols.astype(jnp.float32) * validity[:, None, :], axis=2)

    by_col = jax.vmap(take_slabs)(arrived, col_source) * col_weight[:, :, None, None]
    by_col = by_col.reshape(2, local_cols, row_slots * BLK)
    unflipped = jnp.swapaxes(by_col, 1, 2).reshape(2, row_slots, BLK, local_cols)
    placed = jax.vmap(take_slabs)(unflipped, row_source) * row_weight[:, :, None, None]
    placed = placed.reshape(2, local_rows, local_cols)
    extended = front_matrix + placed[0] + placed[1]

    panel_width = PANEL // BLK
    spread = col_count // panel_width
    lead = extended[:, :BLK]
    lifted = lax.ppermute(
        lead, "col", [(c, c + panel_width * s) for s in range(1, spread) for c in range(panel_width)]
    )
    mine = jnp.where(col_place < panel_width, lead, lifted)
    part_rows = local_rows // spread
    part = lax.dynamic_slice_in_dim(mine, (col_place // panel_width) * part_rows, part_rows, axis=0)
    part = part.reshape(part_rows * BLK // 128, 128)
    gathered = lax.all_gather(part, "col", axis=0, tiled=False)
    gathered = gathered.reshape(spread, panel_width, part_rows, BLK)
    panel_cols = gathered.transpose(0, 2, 1, 3).reshape(local_rows, PANEL)

    corner = lax.all_gather(panel_cols[: PANEL // row_count], "row", axis=0, tiled=True)
    lower_factor = jnp.linalg.cholesky(corner)
    inverse = jax.scipy.linalg.solve_triangular(
        lower_factor, jnp.eye(PANEL, dtype=lower_factor.dtype), lower=True
    )
    solved = jnp.einsum("rp,qp->rq", panel_cols, inverse, precision=exact_mode)
    logical_blk = jnp.arange(row_blocks) * row_count + row_place
    factor_blocks = lower_factor.reshape(panel_width, BLK, PANEL)
    picked = jnp.take(factor_blocks, jnp.minimum(logical_blk, panel_width - 1), axis=0)
    in_panel = (logical_blk < panel_width)[:, None, None]
    panel_factor = jnp.where(in_panel, picked, solved.reshape(row_blocks, BLK, PANEL)).reshape(
        local_rows, PANEL
    )

    ratio = col_count // row_count
    arranged = panel_factor.reshape(col_blocks, ratio, BLK, PANEL)
    chosen = lax.dynamic_index_in_dim(arranged, col_place // row_count, axis=1, keepdims=False)
    chosen = chosen.reshape(col_blocks * BLK, PANEL)
    pairs = []
    for r0 in range(row_count):
        for c1 in range(col_count):
            dest_row = c1 % row_count
            dest_col = r0 + row_count * (c1 // row_count)
            pairs.append((r0 * col_count + c1, dest_row * col_count + dest_col))
    piece_rows = chosen.shape[0] // row_count
    piece = lax.dynamic_slice_in_dim(chosen, (col_place % row_count) * piece_rows, piece_rows, axis=0)
    piece = lax.ppermute(piece, ("row", "col"), pairs)
    across = lax.all_gather(piece, "row", axis=0, tiled=True)
    update = jnp.einsum("rp,cp->rc", panel_factor, across, precision=exact_mode)
    logical_row = jnp.arange(local_rows) // BLK * row_count + row_place
    logical_col = jnp.arange(local_cols) // BLK * col_count + col_place
    retained = (logical_row >= panel_width)[:, None] & (logical_col >= panel_width)[None, :]
    trailing = jnp.where(retained, extended - update, jnp.zeros_like(update))
    return (trailing, panel_factor)


def solution(mesh):
    in_specs = (P("row", "col"), P(None, "row", "col"), P(), P())
    out_specs = (P("row", "col"), P("row", None))
    return jax.shard_map(
        on_device, mesh=mesh, in_specs=in_specs, out_specs=out_specs, check_vma=False
    )
```

```python
import jax
import jax.numpy as jnp
from jax import lax
from jax.sharding import PartitionSpec as P

CHILD = 8192
PANEL = 512
BLK = 64


exact_mode = lax.Precision.HIGHEST


def take_slabs(source, indices):
    return jnp.take(source, indices, axis=0)


def on_device(front_matrix, child_schur, child_index, child_valid):
    row_count = lax.axis_size("row")
    col_count = lax.axis_size("col")
    row_place = lax.axis_index("row")
    col_place = lax.axis_index("col")
    local_rows, local_cols = front_matrix.shape
    row_blocks = local_rows // BLK
    col_blocks = local_cols // BLK
    child_blocks = CHILD // BLK
    child_rowblk = child_schur.shape[1] // BLK
    child_colblk = child_schur.shape[2] // BLK
    per_owner = child_blocks // (row_count * row_count)
    col_multi = max(1, child_blocks // (col_count * col_count))
    row_slots = row_count * per_owner
    col_slots = col_count * col_multi
    validity = child_valid.astype(jnp.float32)
    all_blocks = jnp.arange(child_blocks)
    owner_row = child_index % row_count
    owner_col = child_index % col_count
    sender_row = all_blocks % row_count
    sender_col = all_blocks % col_count
    before = all_blocks[None, :] < all_blocks[:, None]
    earlier_row = (sender_row[:, None] == sender_row[None, :]) & before
    earlier_col = (sender_col[:, None] == sender_col[None, :]) & before
    row_rank = jnp.sum(
        (earlier_row[None] & (owner_row[:, :, None] == owner_row[:, None, :])).astype(jnp.int32),
        axis=2,
    )
    col_rank = jnp.sum(
        (earlier_col[None] & (owner_col[:, :, None] == owner_col[:, None, :])).astype(jnp.int32),
        axis=2,
    )
    row_key = owner_row * per_owner + row_rank
    col_key = owner_col * col_multi + col_rank
    local_arow = row_place + row_count * jnp.arange(child_rowblk)
    mine_rowkey = jnp.take(row_key, local_arow, axis=1)
    row_hit_send = mine_rowkey[:, :, None] == jnp.arange(row_slots)[None, None, :]
    src_row = jnp.sum(
        row_hit_send.astype(jnp.int32) * jnp.arange(child_rowblk)[None, :, None], axis=1
    )
    local_bcol = col_place + col_count * jnp.arange(child_colblk)
    mine_colkey = jnp.take(col_key, local_bcol, axis=1)
    col_hit_send = mine_colkey[:, :, None] == jnp.arange(col_slots)[None, None, :]
    src_col = jnp.sum(
        col_hit_send.astype(jnp.int32) * jnp.arange(child_colblk)[None, :, None], axis=1
    )
    has_col = jnp.sum(col_hit_send.astype(jnp.float32), axis=1)

    panel_width = PANEL // BLK
    corner_blk = jnp.arange(panel_width)
    row_hit = (jnp.take(child_index, local_arow, axis=1)[:, None, :] == corner_blk[None, :, None])
    corner_rpick = jnp.sum(row_hit.astype(jnp.int32) * jnp.arange(child_rowblk)[None, None, :], axis=2)
    corner_rw = jnp.sum(
        row_hit.astype(jnp.float32) * jnp.take(validity, local_arow, axis=1)[:, None, :], axis=2
    )
    col_hit = (jnp.take(child_index, local_bcol, axis=1)[:, None, :] == corner_blk[None, :, None])
    corner_cpick = jnp.sum(col_hit.astype(jnp.int32) * jnp.arange(child_colblk)[None, None, :], axis=2)
    corner_cw = jnp.sum(
        col_hit.astype(jnp.float32) * jnp.take(validity, local_bcol, axis=1)[:, None, :], axis=2
    )
    own = jnp.where(col_place < panel_width, front_matrix[:BLK, :BLK], jnp.zeros((BLK, BLK), jnp.float32))
    partial = lax.dynamic_update_slice(
        jnp.zeros((PANEL, PANEL), jnp.float32),
        own,
        (row_place * BLK, jnp.minimum(col_place, panel_width - 1) * BLK),
    )
    for k in range(2):
        rows_k = take_slabs(child_schur[k].reshape(child_rowblk, BLK, -1), corner_rpick[k])
        rows_k = (rows_k * corner_rw[k][:, None, None]).reshape(PANEL, child_colblk, BLK)
        cols_k = jnp.take(rows_k, corner_cpick[k], axis=1) * corner_cw[k][None, :, None]
        partial = partial + cols_k.reshape(PANEL, PANEL)
    corner = lax.psum(partial, ("row", "col"))

    blocks = child_schur.reshape(2, child_rowblk, BLK, child_colblk * BLK)
    arrived = []
    for k in range(2):
        outgoing = take_slabs(blocks[k], src_row[k]).reshape(row_slots * BLK, child_colblk * BLK)
        if k == 0:
            outgoing, corner = lax.optimization_barrier((outgoing, corner))
            lower_factor = jnp.linalg.cholesky(corner)
            inverse = jax.scipy.linalg.solve_triangular(
                lower_factor, jnp.eye(PANEL, dtype=lower_factor.dtype), lower=True
            )
        section_one = lax.all_to_all(outgoing, "row", split_axis=0, concat_axis=0, tiled=True)
        flipped = section_one.T.reshape(child_colblk, BLK, row_slots * BLK)
        onward = take_slabs(flipped, src_col[k]) * has_col[k][:, None, None]
        onward = onward.reshape(col_slots * BLK, row_slots * BLK)
        section_two = lax.all_to_all(onward, "col", split_axis=0, concat_axis=0, tiled=True)
        if k == 1:
            section_two, lower_factor, inverse = lax.optimization_barrier(
                (section_two, lower_factor, inverse)
            )
        arrived.append(section_two.reshape(col_slots, BLK, row_slots * BLK))
    arrived = jnp.stack(arrived)

    front_rowblk = row_place + row_count * jnp.arange(row_blocks)
    match_rows = (child_index[:, None, :] == front_rowblk[None, :, None]).astype(jnp.int32)
    row_slot_of = sender_row[None, :] * per_owner + row_rank
    row_source = jnp.sum(match_rows * row_slot_of[:, None, :], axis=2)
    row_weight = jnp.sum(match_rows.astype(jnp.float32) * validity[:, None, :], axis=2)
    front_colblk = col_place + col_count * jnp.arange(col_blocks)
    match_cols = (child_index[:, None, :] == front_colblk[None, :, None]).astype(jnp.int32)
    col_slot_of = sender_col[None, :] * col_multi + col_rank
    col_source = jnp.sum(match_cols * col_slot_of[:, None, :], axis=2)
    col_weight = jnp.sum(match_cols.astype(jnp.float32) * validity[:, None, :], axis=2)

    by_col = jax.vmap(take_slabs)(arrived, col_source) * col_weight[:, :, None, None]
    by_col = by_col.reshape(2, local_cols, row_slots * BLK)
    unflipped = jnp.swapaxes(by_col, 1, 2).reshape(2, row_slots, BLK, local_cols)
    placed = jax.vmap(take_slabs)(unflipped, row_source) * row_weight[:, :, None, None]
    placed = placed.reshape(2, local_rows, local_cols)
    extended = front_matrix + placed[0] + placed[1]

    spread = col_count // panel_width
    lead = extended[:, :BLK]
    lifted = lax.ppermute(
        lead, "col", [(c, c + panel_width * s) for s in range(1, spread) for c in range(panel_width)]
    )
    mine = jnp.where(col_place < panel_width, lead, lifted)
    part_rows = local_rows // spread
    part = lax.dynamic_slice_in_dim(mine, (col_place // panel_width) * part_rows, part_rows, axis=0)
    part = part.reshape(part_rows * BLK // 128, 128)
    gathered = lax.all_gather(part, "col", axis=0, tiled=False)
    gathered = gathered.reshape(spread, panel_width, part_rows, BLK)
    panel_cols = gathered.transpose(0, 2, 1, 3).reshape(local_rows, PANEL)

    solved = jnp.einsum("rp,qp->rq", panel_cols, inverse, precision=exact_mode)
    logical_blk = jnp.arange(row_blocks) * row_count + row_place
    factor_blocks = lower_factor.reshape(panel_width, BLK, PANEL)
    picked = jnp.take(factor_blocks, jnp.minimum(logical_blk, panel_width - 1), axis=0)
    in_panel = (logical_blk < panel_width)[:, None, None]
    panel_factor = jnp.where(in_panel, picked, solved.reshape(row_blocks, BLK, PANEL)).reshape(
        local_rows, PANEL
    )

    ratio = col_count // row_count
    arranged = panel_factor.reshape(col_blocks, ratio, BLK, PANEL)
    chosen = lax.dynamic_index_in_dim(arranged, col_place // row_count, axis=1, keepdims=False)
    chosen = chosen.reshape(col_blocks * BLK, PANEL)
    pairs = []
    for r0 in range(row_count):
        for c1 in range(col_count):
            dest_row = c1 % row_count
            dest_col = r0 + row_count * (c1 // row_count)
            pairs.append((r0 * col_count + c1, dest_row * col_count + dest_col))
    piece_rows = chosen.shape[0] // row_count
    piece = lax.dynamic_slice_in_dim(chosen, (col_place % row_count) * piece_rows, piece_rows, axis=0)
    piece = lax.ppermute(piece, ("row", "col"), pairs)
    across = lax.all_gather(piece, "row", axis=0, tiled=True)
    update = jnp.einsum("rp,cp->rc", panel_factor, across, precision=exact_mode)
    logical_row = jnp.arange(local_rows) // BLK * row_count + row_place
    logical_col = jnp.arange(local_cols) // BLK * col_count + col_place
    retained = (logical_row >= panel_width)[:, None] & (logical_col >= panel_width)[None, :]
    trailing = jnp.where(retained, extended - update, jnp.zeros_like(update))
    return (trailing, panel_factor)


def solution(mesh):
    in_specs = (P("row", "col"), P(None, "row", "col"), P(), P())
    out_specs = (P("row", "col"), P("row", None))
    return jax.shard_map(
        on_device, mesh=mesh, in_specs=in_specs, out_specs=out_specs, check_vma=False
    )
```

```python
import jax
import jax.numpy as jnp
from jax import lax
from jax.sharding import PartitionSpec as P

CHILD = 8192
PANEL = 512
BLK = 64


exact_mode = lax.Precision.HIGHEST


def take_slabs(source, indices):
    return jnp.take(source, indices, axis=0)


def on_device(front_matrix, child_schur, child_index, child_valid):
    row_count = lax.axis_size("row")
    col_count = lax.axis_size("col")
    row_place = lax.axis_index("row")
    col_place = lax.axis_index("col")
    local_rows, local_cols = front_matrix.shape
    row_blocks = local_rows // BLK
    col_blocks = local_cols // BLK
    child_blocks = CHILD // BLK
    child_rowblk = child_schur.shape[1] // BLK
    child_colblk = child_schur.shape[2] // BLK
    per_owner = child_blocks // (row_count * row_count)
    col_multi = max(1, child_blocks // (col_count * col_count))
    row_slots = row_count * per_owner
    col_slots = col_count * col_multi
    validity = child_valid.astype(jnp.float32)
    all_blocks = jnp.arange(child_blocks)
    owner_row = child_index % row_count
    owner_col = child_index % col_count
    sender_row = all_blocks % row_count
    sender_col = all_blocks % col_count
    before = all_blocks[None, :] < all_blocks[:, None]
    earlier_row = (sender_row[:, None] == sender_row[None, :]) & before
    earlier_col = (sender_col[:, None] == sender_col[None, :]) & before
    row_rank = jnp.sum(
        (earlier_row[None] & (owner_row[:, :, None] == owner_row[:, None, :])).astype(jnp.int32),
        axis=2,
    )
    col_rank = jnp.sum(
        (earlier_col[None] & (owner_col[:, :, None] == owner_col[:, None, :])).astype(jnp.int32),
        axis=2,
    )
    row_key = owner_row * per_owner + row_rank
    col_key = owner_col * col_multi + col_rank
    local_arow = row_place + row_count * jnp.arange(child_rowblk)
    mine_rowkey = jnp.take(row_key, local_arow, axis=1)
    row_hit_send = mine_rowkey[:, :, None] == jnp.arange(row_slots)[None, None, :]
    src_row = jnp.sum(
        row_hit_send.astype(jnp.int32) * jnp.arange(child_rowblk)[None, :, None], axis=1
    )
    local_bcol = col_place + col_count * jnp.arange(child_colblk)
    mine_colkey = jnp.take(col_key, local_bcol, axis=1)
    col_hit_send = mine_colkey[:, :, None] == jnp.arange(col_slots)[None, None, :]
    src_col = jnp.sum(
        col_hit_send.astype(jnp.int32) * jnp.arange(child_colblk)[None, :, None], axis=1
    )
    has_col = jnp.sum(col_hit_send.astype(jnp.float32), axis=1)

    front_rowblk = row_place + row_count * jnp.arange(row_blocks)
    match_rows = (child_index[:, None, :] == front_rowblk[None, :, None]).astype(jnp.int32)
    row_slot_of = sender_row[None, :] * per_owner + row_rank
    row_source = jnp.sum(match_rows * row_slot_of[:, None, :], axis=2)
    row_weight = jnp.sum(match_rows.astype(jnp.float32) * validity[:, None, :], axis=2)
    front_colblk = col_place + col_count * jnp.arange(col_blocks)
    match_cols = (child_index[:, None, :] == front_colblk[None, :, None]).astype(jnp.int32)
    col_slot_of = sender_col[None, :] * col_multi + col_rank
    col_source = jnp.sum(match_cols * col_slot_of[:, None, :], axis=2)
    col_weight = jnp.sum(match_cols.astype(jnp.float32) * validity[:, None, :], axis=2)

    blocks = child_schur.reshape(2, child_rowblk, BLK, child_colblk * BLK)
    section_one = []
    for k in range(2):
        outgoing = take_slabs(blocks[k], src_row[k]).reshape(row_slots * BLK, child_colblk * BLK)
        section_one.append(lax.all_to_all(outgoing, "row", split_axis=0, concat_axis=0, tiled=True))

    panel_width = PANEL // BLK
    corner_blk = jnp.arange(panel_width)
    col_hit = (jnp.take(child_index, local_bcol, axis=1)[:, None, :] == corner_blk[None, :, None])
    corner_cpick = jnp.sum(col_hit.astype(jnp.int32) * jnp.arange(child_colblk)[None, None, :], axis=2)
    corner_cw = jnp.sum(
        col_hit.astype(jnp.float32) * jnp.take(validity, local_bcol, axis=1)[:, None, :], axis=2
    )
    own = jnp.where(col_place < panel_width, front_matrix[:BLK, :BLK], jnp.zeros((BLK, BLK), jnp.float32))
    partial = lax.dynamic_update_slice(
        jnp.zeros((BLK, PANEL), jnp.float32), own, (0, jnp.minimum(col_place, panel_width - 1) * BLK)
    )
    for k in range(2):
        slab = lax.dynamic_slice_in_dim(section_one[k], row_source[k, 0] * BLK, BLK, axis=0)
        slab = (slab * row_weight[k, 0]).reshape(BLK, child_colblk, BLK)
        picked_cols = jnp.take(slab, corner_cpick[k], axis=1) * corner_cw[k][None, :, None]
        partial = partial + picked_cols.reshape(BLK, PANEL)
    corner_row = lax.psum(partial, "col")
    corner = lax.all_gather(corner_row, "row", axis=0, tiled=True)

    arrived = []
    for k in range(2):
        flipped = section_one[k].T.reshape(child_colblk, BLK, row_slots * BLK)
        onward = take_slabs(flipped, src_col[k]) * has_col[k][:, None, None]
        onward = onward.reshape(col_slots * BLK, row_slots * BLK)
        if k == 0:
            onward, corner = lax.optimization_barrier((onward, corner))
            lower_factor = jnp.linalg.cholesky(corner)
            inverse = jax.scipy.linalg.solve_triangular(
                lower_factor, jnp.eye(PANEL, dtype=lower_factor.dtype), lower=True
            )
        section_two = lax.all_to_all(onward, "col", split_axis=0, concat_axis=0, tiled=True)
        if k == 1:
            section_two, lower_factor, inverse = lax.optimization_barrier(
                (section_two, lower_factor, inverse)
            )
        arrived.append(section_two.reshape(col_slots, BLK, row_slots * BLK))
    arrived = jnp.stack(arrived)

    by_col = jax.vmap(take_slabs)(arrived, col_source) * col_weight[:, :, None, None]
    by_col = by_col.reshape(2, local_cols, row_slots * BLK)
    unflipped = jnp.swapaxes(by_col, 1, 2).reshape(2, row_slots, BLK, local_cols)
    placed = jax.vmap(take_slabs)(unflipped, row_source) * row_weight[:, :, None, None]
    placed = placed.reshape(2, local_rows, local_cols)
    extended = front_matrix + placed[0] + placed[1]

    spread = col_count // panel_width
    lead = extended[:, :BLK]
    lifted = lax.ppermute(
        lead, "col", [(c, c + panel_width * s) for s in range(1, spread) for c in range(panel_width)]
    )
    mine = jnp.where(col_place < panel_width, lead, lifted)
    part_rows = local_rows // spread
    part = lax.dynamic_slice_in_dim(mine, (col_place // panel_width) * part_rows, part_rows, axis=0)
    part = part.reshape(part_rows * BLK // 128, 128)
    gathered = lax.all_gather(part, "col", axis=0, tiled=False)
    gathered = gathered.reshape(spread, panel_width, part_rows, BLK)
    panel_cols = gathered.transpose(0, 2, 1, 3).reshape(local_rows, PANEL)

    solved = jnp.einsum("rp,qp->rq", panel_cols, inverse, precision=exact_mode)
    logical_blk = jnp.arange(row_blocks) * row_count + row_place
    factor_blocks = lower_factor.reshape(panel_width, BLK, PANEL)
    picked = jnp.take(factor_blocks, jnp.minimum(logical_blk, panel_width - 1), axis=0)
    in_panel = (logical_blk < panel_width)[:, None, None]
    panel_factor = jnp.where(in_panel, picked, solved.reshape(row_blocks, BLK, PANEL)).reshape(
        local_rows, PANEL
    )

    ratio = col_count // row_count
    arranged = panel_factor.reshape(col_blocks, ratio, BLK, PANEL)
    chosen = lax.dynamic_index_in_dim(arranged, col_place // row_count, axis=1, keepdims=False)
    chosen = chosen.reshape(col_blocks * BLK, PANEL)
    pairs = []
    for r0 in range(row_count):
        for c1 in range(col_count):
            dest_row = c1 % row_count
            dest_col = r0 + row_count * (c1 // row_count)
            pairs.append((r0 * col_count + c1, dest_row * col_count + dest_col))
    piece_rows = chosen.shape[0] // row_count
    piece = lax.dynamic_slice_in_dim(chosen, (col_place % row_count) * piece_rows, piece_rows, axis=0)
    piece = lax.ppermute(piece, ("row", "col"), pairs)
    across = lax.all_gather(piece, "row", axis=0, tiled=True)
    update = jnp.einsum("rp,cp->rc", panel_factor, across, precision=exact_mode)
    logical_row = jnp.arange(local_rows) // BLK * row_count + row_place
    logical_col = jnp.arange(local_cols) // BLK * col_count + col_place
    retained = (logical_row >= panel_width)[:, None] & (logical_col >= panel_width)[None, :]
    trailing = jnp.where(retained, extended - update, jnp.zeros_like(update))
    return (trailing, panel_factor)


def solution(mesh):
    in_specs = (P("row", "col"), P(None, "row", "col"), P(), P())
    out_specs = (P("row", "col"), P("row", None))
    return jax.shard_map(
        on_device, mesh=mesh, in_specs=in_specs, out_specs=out_specs, check_vma=False
    )
```

```python
import jax
import jax.numpy as jnp
from jax import lax
from jax.sharding import PartitionSpec as P

CHILD = 8192
PANEL = 512
BLK = 64


exact_mode = lax.Precision.HIGHEST


def take_slabs(source, indices):
    return jnp.take(source, indices, axis=0)


def on_device(front_matrix, child_schur, child_index, child_valid):
    row_count = lax.axis_size("row")
    col_count = lax.axis_size("col")
    row_place = lax.axis_index("row")
    col_place = lax.axis_index("col")
    local_rows, local_cols = front_matrix.shape
    row_blocks = local_rows // BLK
    col_blocks = local_cols // BLK
    child_blocks = CHILD // BLK
    child_rowblk = child_schur.shape[1] // BLK
    child_colblk = child_schur.shape[2] // BLK
    per_owner = child_blocks // (row_count * row_count)
    col_multi = max(1, child_blocks // (col_count * col_count))
    row_slots = row_count * per_owner
    col_slots = col_count * col_multi
    validity = child_valid.astype(jnp.float32)
    all_blocks = jnp.arange(child_blocks)
    owner_row = child_index % row_count
    owner_col = child_index % col_count
    sender_row = all_blocks % row_count
    sender_col = all_blocks % col_count
    before = all_blocks[None, :] < all_blocks[:, None]
    earlier_row = (sender_row[:, None] == sender_row[None, :]) & before
    earlier_col = (sender_col[:, None] == sender_col[None, :]) & before
    row_rank = jnp.sum(
        (earlier_row[None] & (owner_row[:, :, None] == owner_row[:, None, :])).astype(jnp.int32),
        axis=2,
    )
    col_rank = jnp.sum(
        (earlier_col[None] & (owner_col[:, :, None] == owner_col[:, None, :])).astype(jnp.int32),
        axis=2,
    )
    row_key = owner_row * per_owner + row_rank
    col_key = owner_col * col_multi + col_rank
    local_arow = row_place + row_count * jnp.arange(child_rowblk)
    mine_rowkey = jnp.take(row_key, local_arow, axis=1)
    row_hit_send = mine_rowkey[:, :, None] == jnp.arange(row_slots)[None, None, :]
    src_row = jnp.sum(
        row_hit_send.astype(jnp.int32) * jnp.arange(child_rowblk)[None, :, None], axis=1
    )
    local_bcol = col_place + col_count * jnp.arange(child_colblk)
    mine_colkey = jnp.take(col_key, local_bcol, axis=1)
    col_hit_send = mine_colkey[:, :, None] == jnp.arange(col_slots)[None, None, :]
    src_col = jnp.sum(
        col_hit_send.astype(jnp.int32) * jnp.arange(child_colblk)[None, :, None], axis=1
    )
    has_col = jnp.sum(col_hit_send.astype(jnp.float32), axis=1)

    front_rowblk = row_place + row_count * jnp.arange(row_blocks)
    match_rows = (child_index[:, None, :] == front_rowblk[None, :, None]).astype(jnp.int32)
    row_slot_of = sender_row[None, :] * per_owner + row_rank
    row_source = jnp.sum(match_rows * row_slot_of[:, None, :], axis=2)
    row_weight = jnp.sum(match_rows.astype(jnp.float32) * validity[:, None, :], axis=2)
    front_colblk = col_place + col_count * jnp.arange(col_blocks)
    match_cols = (child_index[:, None, :] == front_colblk[None, :, None]).astype(jnp.int32)
    col_slot_of = sender_col[None, :] * col_multi + col_rank
    col_source = jnp.sum(match_cols * col_slot_of[:, None, :], axis=2)
    col_weight = jnp.sum(match_cols.astype(jnp.float32) * validity[:, None, :], axis=2)

    blocks = child_schur.reshape(2, child_rowblk, BLK, child_colblk * BLK)
    section_one = []
    for k in range(2):
        outgoing = take_slabs(blocks[k], src_row[k]).reshape(row_slots * BLK, child_colblk * BLK)
        section_one.append(lax.all_to_all(outgoing, "row", split_axis=0, concat_axis=0, tiled=True))

    panel_width = PANEL // BLK
    corner_blk = jnp.arange(panel_width)
    col_hit = (jnp.take(child_index, local_bcol, axis=1)[:, None, :] == corner_blk[None, :, None])
    corner_cpick = jnp.sum(col_hit.astype(jnp.int32) * jnp.arange(child_colblk)[None, None, :], axis=2)
    corner_cw = jnp.sum(
        col_hit.astype(jnp.float32) * jnp.take(validity, local_bcol, axis=1)[:, None, :], axis=2
    )
    own = jnp.where(col_place < panel_width, front_matrix[:BLK, :BLK], jnp.zeros((BLK, BLK), jnp.float32))
    partial = lax.dynamic_update_slice(
        jnp.zeros((BLK, PANEL), jnp.float32), own, (0, jnp.minimum(col_place, panel_width - 1) * BLK)
    )
    for k in range(2):
        slab = lax.dynamic_slice_in_dim(section_one[k], row_source[k, 0] * BLK, BLK, axis=0)
        slab = (slab * row_weight[k, 0]).reshape(BLK, child_colblk, BLK)
        picked_cols = jnp.take(slab, corner_cpick[k], axis=1) * corner_cw[k][None, :, None]
        partial = partial + picked_cols.reshape(BLK, PANEL)
    corner_row = jnp.sum(lax.all_gather(partial, "col", axis=0, tiled=False), axis=0)
    corner = lax.all_gather(corner_row, "row", axis=0, tiled=True)

    arrived = []
    for k in range(2):
        flipped = section_one[k].T.reshape(child_colblk, BLK, row_slots * BLK)
        onward = take_slabs(flipped, src_col[k]) * has_col[k][:, None, None]
        onward = onward.reshape(col_slots * BLK, row_slots * BLK)
        if k == 0:
            onward, corner = lax.optimization_barrier((onward, corner))
            lower_factor = jnp.linalg.cholesky(corner)
            inverse = jax.scipy.linalg.solve_triangular(
                lower_factor, jnp.eye(PANEL, dtype=lower_factor.dtype), lower=True
            )
        section_two = lax.all_to_all(onward, "col", split_axis=0, concat_axis=0, tiled=True)
        if k == 1:
            section_two, lower_factor, inverse = lax.optimization_barrier(
                (section_two, lower_factor, inverse)
            )
        arrived.append(section_two.reshape(col_slots, BLK, row_slots * BLK))
    arrived = jnp.stack(arrived)

    by_col = jax.vmap(take_slabs)(arrived, col_source) * col_weight[:, :, None, None]
    by_col = by_col.reshape(2, local_cols, row_slots * BLK)
    unflipped = jnp.swapaxes(by_col, 1, 2).reshape(2, row_slots, BLK, local_cols)
    placed = jax.vmap(take_slabs)(unflipped, row_source) * row_weight[:, :, None, None]
    placed = placed.reshape(2, local_rows, local_cols)
    extended = front_matrix + placed[0] + placed[1]

    spread = col_count // panel_width
    lead = front_matrix[:, :BLK]
    for k in range(2):
        first_col = lax.dynamic_index_in_dim(arrived[k], col_source[k, 0], axis=0, keepdims=False)
        first_col = (first_col * col_weight[k, 0]).T.reshape(row_slots, BLK, BLK)
        lead = lead + (take_slabs(first_col, row_source[k]) * row_weight[k][:, None, None]).reshape(
            local_rows, BLK
        )
    lifted = lax.ppermute(
        lead, "col", [(c, c + panel_width * s) for s in range(1, spread) for c in range(panel_width)]
    )
    mine = jnp.where(col_place < panel_width, lead, lifted)
    part_rows = local_rows // spread
    part = lax.dynamic_slice_in_dim(mine, (col_place // panel_width) * part_rows, part_rows, axis=0)
    part = part.reshape(part_rows * BLK // 128, 128)
    gathered = lax.all_gather(part, "col", axis=0, tiled=False)
    gathered = gathered.reshape(spread, panel_width, part_rows, BLK)
    panel_cols = gathered.transpose(0, 2, 1, 3).reshape(local_rows, PANEL)

    solved = jnp.einsum("rp,qp->rq", panel_cols, inverse, precision=exact_mode)
    logical_blk = jnp.arange(row_blocks) * row_count + row_place
    factor_blocks = lower_factor.reshape(panel_width, BLK, PANEL)
    picked = jnp.take(factor_blocks, jnp.minimum(logical_blk, panel_width - 1), axis=0)
    in_panel = (logical_blk < panel_width)[:, None, None]
    panel_factor = jnp.where(in_panel, picked, solved.reshape(row_blocks, BLK, PANEL)).reshape(
        local_rows, PANEL
    )

    ratio = col_count // row_count
    arranged = panel_factor.reshape(col_blocks, ratio, BLK, PANEL)
    chosen = lax.dynamic_index_in_dim(arranged, col_place // row_count, axis=1, keepdims=False)
    chosen = chosen.reshape(col_blocks * BLK, PANEL)
    pairs = []
    for r0 in range(row_count):
        for c1 in range(col_count):
            dest_row = c1 % row_count
            dest_col = r0 + row_count * (c1 // row_count)
            pairs.append((r0 * col_count + c1, dest_row * col_count + dest_col))
    piece_rows = chosen.shape[0] // row_count
    piece = lax.dynamic_slice_in_dim(chosen, (col_place % row_count) * piece_rows, piece_rows, axis=0)
    piece = lax.ppermute(piece, ("row", "col"), pairs)
    across = lax.all_gather(piece, "row", axis=0, tiled=True)
    update = jnp.einsum("rp,cp->rc", panel_factor, across, precision=exact_mode)
    logical_row = jnp.arange(local_rows) // BLK * row_count + row_place
    logical_col = jnp.arange(local_cols) // BLK * col_count + col_place
    retained = (logical_row >= panel_width)[:, None] & (logical_col >= panel_width)[None, :]
    trailing = jnp.where(retained, extended - update, jnp.zeros_like(update))
    return (trailing, panel_factor)


def solution(mesh):
    in_specs = (P("row", "col"), P(None, "row", "col"), P(), P())
    out_specs = (P("row", "col"), P("row", None))
    return jax.shard_map(
        on_device, mesh=mesh, in_specs=in_specs, out_specs=out_specs, check_vma=False
    )
```

```python
import jax
import jax.numpy as jnp
from jax import lax
from jax.sharding import PartitionSpec as P

CHILD = 8192
PANEL = 512
BLK = 64


exact_mode = lax.Precision.HIGHEST


def take_slabs(source, indices):
    return jnp.take(source, indices, axis=0)


def factor_and_invert(corner, width=128):
    count = corner.shape[0] // width
    sym = (corner + corner.T) / 2
    grid = [[sym[i * width : (i + 1) * width, j * width : (j + 1) * width] for j in range(count)] for i in range(count)]
    eye = jnp.eye(width, dtype=corner.dtype)
    low = [[None] * count for _ in range(count)]
    diag_inv = []
    for p in range(count):
        lpp = lax.linalg.cholesky(grid[p][p], symmetrize_input=False)
        dinv = jax.scipy.linalg.solve_triangular(lpp, eye, lower=True)
        low[p][p] = lpp
        diag_inv.append(dinv)
        for i in range(p + 1, count):
            low[i][p] = jnp.dot(grid[i][p], dinv.T, precision=exact_mode)
        for i in range(p + 1, count):
            for j in range(p + 1, i + 1):
                grid[i][j] = grid[i][j] - jnp.dot(low[i][p], low[j][p].T, precision=exact_mode)
    zero = jnp.zeros((width, width), corner.dtype)
    inv = [[zero] * count for _ in range(count)]
    for j in range(count):
        inv[j][j] = diag_inv[j]
        for i in range(j + 1, count):
            acc = jnp.dot(low[i][j], inv[j][j], precision=exact_mode)
            for k in range(j + 1, i):
                acc = acc + jnp.dot(low[i][k], inv[k][j], precision=exact_mode)
            inv[i][j] = -jnp.dot(diag_inv[i], acc, precision=exact_mode)
    lower = jnp.block([[low[i][j] if j <= i else zero for j in range(count)] for i in range(count)])
    inverse = jnp.block(inv)
    return lower, inverse


def on_device(front_matrix, child_schur, child_index, child_valid):
    row_count = lax.axis_size("row")
    col_count = lax.axis_size("col")
    row_place = lax.axis_index("row")
    col_place = lax.axis_index("col")
    local_rows, local_cols = front_matrix.shape
    row_blocks = local_rows // BLK
    col_blocks = local_cols // BLK
    child_blocks = CHILD // BLK
    child_rowblk = child_schur.shape[1] // BLK
    child_colblk = child_schur.shape[2] // BLK
    per_owner = child_blocks // (row_count * row_count)
    col_multi = max(1, child_blocks // (col_count * col_count))
    row_slots = row_count * per_owner
    col_slots = col_count * col_multi
    validity = child_valid.astype(jnp.float32)
    all_blocks = jnp.arange(child_blocks)
    owner_row = child_index % row_count
    owner_col = child_index % col_count
    sender_row = all_blocks % row_count
    sender_col = all_blocks % col_count
    before = all_blocks[None, :] < all_blocks[:, None]
    earlier_row = (sender_row[:, None] == sender_row[None, :]) & before
    earlier_col = (sender_col[:, None] == sender_col[None, :]) & before
    row_rank = jnp.sum(
        (earlier_row[None] & (owner_row[:, :, None] == owner_row[:, None, :])).astype(jnp.int32),
        axis=2,
    )
    col_rank = jnp.sum(
        (earlier_col[None] & (owner_col[:, :, None] == owner_col[:, None, :])).astype(jnp.int32),
        axis=2,
    )
    row_key = owner_row * per_owner + row_rank
    col_key = owner_col * col_multi + col_rank
    local_arow = row_place + row_count * jnp.arange(child_rowblk)
    mine_rowkey = jnp.take(row_key, local_arow, axis=1)
    row_hit_send = mine_rowkey[:, :, None] == jnp.arange(row_slots)[None, None, :]
    src_row = jnp.sum(
        row_hit_send.astype(jnp.int32) * jnp.arange(child_rowblk)[None, :, None], axis=1
    )
    local_bcol = col_place + col_count * jnp.arange(child_colblk)
    mine_colkey = jnp.take(col_key, local_bcol, axis=1)
    col_hit_send = mine_colkey[:, :, None] == jnp.arange(col_slots)[None, None, :]
    src_col = jnp.sum(
        col_hit_send.astype(jnp.int32) * jnp.arange(child_colblk)[None, :, None], axis=1
    )
    has_col = jnp.sum(col_hit_send.astype(jnp.float32), axis=1)

    front_rowblk = row_place + row_count * jnp.arange(row_blocks)
    match_rows = (child_index[:, None, :] == front_rowblk[None, :, None]).astype(jnp.int32)
    row_slot_of = sender_row[None, :] * per_owner + row_rank
    row_source = jnp.sum(match_rows * row_slot_of[:, None, :], axis=2)
    row_weight = jnp.sum(match_rows.astype(jnp.float32) * validity[:, None, :], axis=2)
    front_colblk = col_place + col_count * jnp.arange(col_blocks)
    match_cols = (child_index[:, None, :] == front_colblk[None, :, None]).astype(jnp.int32)
    col_slot_of = sender_col[None, :] * col_multi + col_rank
    col_source = jnp.sum(match_cols * col_slot_of[:, None, :], axis=2)
    col_weight = jnp.sum(match_cols.astype(jnp.float32) * validity[:, None, :], axis=2)

    blocks = child_schur.reshape(2, child_rowblk, BLK, child_colblk * BLK)
    section_one = []
    for k in range(2):
        outgoing = take_slabs(blocks[k], src_row[k]).reshape(row_slots * BLK, child_colblk * BLK)
        section_one.append(lax.all_to_all(outgoing, "row", split_axis=0, concat_axis=0, tiled=True))

    panel_width = PANEL // BLK
    corner_blk = jnp.arange(panel_width)
    col_hit = (jnp.take(child_index, local_bcol, axis=1)[:, None, :] == corner_blk[None, :, None])
    corner_cpick = jnp.sum(col_hit.astype(jnp.int32) * jnp.arange(child_colblk)[None, None, :], axis=2)
    corner_cw = jnp.sum(
        col_hit.astype(jnp.float32) * jnp.take(validity, local_bcol, axis=1)[:, None, :], axis=2
    )
    own = jnp.where(col_place < panel_width, front_matrix[:BLK, :BLK], jnp.zeros((BLK, BLK), jnp.float32))
    partial = lax.dynamic_update_slice(
        jnp.zeros((BLK, PANEL), jnp.float32), own, (0, jnp.minimum(col_place, panel_width - 1) * BLK)
    )
    for k in range(2):
        slab = lax.dynamic_slice_in_dim(section_one[k], row_source[k, 0] * BLK, BLK, axis=0)
        slab = (slab * row_weight[k, 0]).reshape(BLK, child_colblk, BLK)
        picked_cols = jnp.take(slab, corner_cpick[k], axis=1) * corner_cw[k][None, :, None]
        partial = partial + picked_cols.reshape(BLK, PANEL)
    corner_row = jnp.sum(lax.all_gather(partial, "col", axis=0, tiled=False), axis=0)
    corner = lax.all_gather(corner_row, "row", axis=0, tiled=True)

    arrived = []
    for k in range(2):
        flipped = section_one[k].T.reshape(child_colblk, BLK, row_slots * BLK)
        onward = take_slabs(flipped, src_col[k]) * has_col[k][:, None, None]
        onward = onward.reshape(col_slots * BLK, row_slots * BLK)
        if k == 0:
            onward, corner = lax.optimization_barrier((onward, corner))
            lower_factor, inverse = factor_and_invert(corner)
        section_two = lax.all_to_all(onward, "col", split_axis=0, concat_axis=0, tiled=True)
        if k == 1:
            section_two, lower_factor, inverse = lax.optimization_barrier(
                (section_two, lower_factor, inverse)
            )
        arrived.append(section_two.reshape(col_slots, BLK, row_slots * BLK))
    arrived = jnp.stack(arrived)

    by_col = jax.vmap(take_slabs)(arrived, col_source) * col_weight[:, :, None, None]
    by_col = by_col.reshape(2, local_cols, row_slots * BLK)
    unflipped = jnp.swapaxes(by_col, 1, 2).reshape(2, row_slots, BLK, local_cols)
    placed = jax.vmap(take_slabs)(unflipped, row_source) * row_weight[:, :, None, None]
    placed = placed.reshape(2, local_rows, local_cols)
    extended = front_matrix + placed[0] + placed[1]

    spread = col_count // panel_width
    lead = front_matrix[:, :BLK]
    for k in range(2):
        first_col = lax.dynamic_index_in_dim(arrived[k], col_source[k, 0], axis=0, keepdims=False)
        first_col = (first_col * col_weight[k, 0]).T.reshape(row_slots, BLK, BLK)
        lead = lead + (take_slabs(first_col, row_source[k]) * row_weight[k][:, None, None]).reshape(
            local_rows, BLK
        )
    lifted = lax.ppermute(
        lead, "col", [(c, c + panel_width * s) for s in range(1, spread) for c in range(panel_width)]
    )
    mine = jnp.where(col_place < panel_width, lead, lifted)
    part_rows = local_rows // spread
    part = lax.dynamic_slice_in_dim(mine, (col_place // panel_width) * part_rows, part_rows, axis=0)
    part = part.reshape(part_rows * BLK // 128, 128)
    gathered = lax.all_gather(part, "col", axis=0, tiled=False)
    gathered = gathered.reshape(spread, panel_width, part_rows, BLK)
    panel_cols = gathered.transpose(0, 2, 1, 3).reshape(local_rows, PANEL)

    solved = jnp.einsum("rp,qp->rq", panel_cols, inverse, precision=exact_mode)
    logical_blk = jnp.arange(row_blocks) * row_count + row_place
    factor_blocks = lower_factor.reshape(panel_width, BLK, PANEL)
    picked = jnp.take(factor_blocks, jnp.minimum(logical_blk, panel_width - 1), axis=0)
    in_panel = (logical_blk < panel_width)[:, None, None]
    panel_factor = jnp.where(in_panel, picked, solved.reshape(row_blocks, BLK, PANEL)).reshape(
        local_rows, PANEL
    )

    ratio = col_count // row_count
    arranged = panel_factor.reshape(col_blocks, ratio, BLK, PANEL)
    chosen = lax.dynamic_index_in_dim(arranged, col_place // row_count, axis=1, keepdims=False)
    chosen = chosen.reshape(col_blocks * BLK, PANEL)
    pairs = []
    for r0 in range(row_count):
        for c1 in range(col_count):
            dest_row = c1 % row_count
            dest_col = r0 + row_count * (c1 // row_count)
            pairs.append((r0 * col_count + c1, dest_row * col_count + dest_col))
    piece_rows = chosen.shape[0] // row_count
    piece = lax.dynamic_slice_in_dim(chosen, (col_place % row_count) * piece_rows, piece_rows, axis=0)
    piece = lax.ppermute(piece, ("row", "col"), pairs)
    across = lax.all_gather(piece, "row", axis=0, tiled=True)
    update = jnp.einsum("rp,cp->rc", panel_factor, across, precision=exact_mode)
    logical_row = jnp.arange(local_rows) // BLK * row_count + row_place
    logical_col = jnp.arange(local_cols) // BLK * col_count + col_place
    retained = (logical_row >= panel_width)[:, None] & (logical_col >= panel_width)[None, :]
    trailing = jnp.where(retained, extended - update, jnp.zeros_like(update))
    return (trailing, panel_factor)


def solution(mesh):
    in_specs = (P("row", "col"), P(None, "row", "col"), P(), P())
    out_specs = (P("row", "col"), P("row", None))
    return jax.shard_map(
        on_device, mesh=mesh, in_specs=in_specs, out_specs=out_specs, check_vma=False
    )
```

```python
import jax
import jax.numpy as jnp
from jax import lax
from jax.sharding import PartitionSpec as P

CHILD = 8192
PANEL = 512
BLK = 64


exact_mode = lax.Precision.HIGHEST


def take_slabs(source, indices):
    return jnp.take(source, indices, axis=0)


def factor_and_invert(corner, width=128):
    count = corner.shape[0] // width
    sym = (corner + corner.T) / 2
    grid = [[sym[i * width : (i + 1) * width, j * width : (j + 1) * width] for j in range(count)] for i in range(count)]
    eye = jnp.eye(width, dtype=corner.dtype)
    low = [[None] * count for _ in range(count)]
    diag_inv = []
    for p in range(count):
        lpp = lax.linalg.cholesky(grid[p][p], symmetrize_input=False)
        dinv = jax.scipy.linalg.solve_triangular(lpp, eye, lower=True)
        low[p][p] = lpp
        diag_inv.append(dinv)
        for i in range(p + 1, count):
            low[i][p] = jnp.dot(grid[i][p], dinv.T, precision=exact_mode)
        for i in range(p + 1, count):
            for j in range(p + 1, i + 1):
                grid[i][j] = grid[i][j] - jnp.dot(low[i][p], low[j][p].T, precision=exact_mode)
    zero = jnp.zeros((width, width), corner.dtype)
    inv = [[zero] * count for _ in range(count)]
    for j in range(count):
        inv[j][j] = diag_inv[j]
        for i in range(j + 1, count):
            acc = jnp.dot(low[i][j], inv[j][j], precision=exact_mode)
            for k in range(j + 1, i):
                acc = acc + jnp.dot(low[i][k], inv[k][j], precision=exact_mode)
            inv[i][j] = -jnp.dot(diag_inv[i], acc, precision=exact_mode)
    lower = jnp.block([[low[i][j] if j <= i else zero for j in range(count)] for i in range(count)])
    inverse = jnp.block(inv)
    return lower, inverse


def on_device(front_matrix, child_schur, child_index, child_valid):
    row_count = lax.axis_size("row")
    col_count = lax.axis_size("col")
    row_place = lax.axis_index("row")
    col_place = lax.axis_index("col")
    local_rows, local_cols = front_matrix.shape
    row_blocks = local_rows // BLK
    col_blocks = local_cols // BLK
    child_blocks = CHILD // BLK
    child_rowblk = child_schur.shape[1] // BLK
    child_colblk = child_schur.shape[2] // BLK
    per_owner = child_blocks // (row_count * row_count)
    col_multi = max(1, child_blocks // (col_count * col_count))
    row_slots = row_count * per_owner
    col_slots = col_count * col_multi
    validity = child_valid.astype(jnp.float32)
    all_blocks = jnp.arange(child_blocks)
    owner_row = child_index % row_count
    owner_col = child_index % col_count
    sender_row = all_blocks % row_count
    sender_col = all_blocks % col_count
    before = all_blocks[None, :] < all_blocks[:, None]
    earlier_row = (sender_row[:, None] == sender_row[None, :]) & before
    earlier_col = (sender_col[:, None] == sender_col[None, :]) & before
    row_rank = jnp.sum(
        (earlier_row[None] & (owner_row[:, :, None] == owner_row[:, None, :])).astype(jnp.int32),
        axis=2,
    )
    col_rank = jnp.sum(
        (earlier_col[None] & (owner_col[:, :, None] == owner_col[:, None, :])).astype(jnp.int32),
        axis=2,
    )
    row_key = owner_row * per_owner + row_rank
    col_key = owner_col * col_multi + col_rank
    local_arow = row_place + row_count * jnp.arange(child_rowblk)
    mine_rowkey = jnp.take(row_key, local_arow, axis=1)
    row_hit_send = mine_rowkey[:, :, None] == jnp.arange(row_slots)[None, None, :]
    src_row = jnp.sum(
        row_hit_send.astype(jnp.int32) * jnp.arange(child_rowblk)[None, :, None], axis=1
    )
    local_bcol = col_place + col_count * jnp.arange(child_colblk)
    mine_colkey = jnp.take(col_key, local_bcol, axis=1)
    col_hit_send = mine_colkey[:, :, None] == jnp.arange(col_slots)[None, None, :]
    src_col = jnp.sum(
        col_hit_send.astype(jnp.int32) * jnp.arange(child_colblk)[None, :, None], axis=1
    )
    has_col = jnp.sum(col_hit_send.astype(jnp.float32), axis=1)

    front_rowblk = row_place + row_count * jnp.arange(row_blocks)
    match_rows = (child_index[:, None, :] == front_rowblk[None, :, None]).astype(jnp.int32)
    row_slot_of = sender_row[None, :] * per_owner + row_rank
    row_source = jnp.sum(match_rows * row_slot_of[:, None, :], axis=2)
    row_weight = jnp.sum(match_rows.astype(jnp.float32) * validity[:, None, :], axis=2)
    front_colblk = col_place + col_count * jnp.arange(col_blocks)
    match_cols = (child_index[:, None, :] == front_colblk[None, :, None]).astype(jnp.int32)
    col_slot_of = sender_col[None, :] * col_multi + col_rank
    col_source = jnp.sum(match_cols * col_slot_of[:, None, :], axis=2)
    col_weight = jnp.sum(match_cols.astype(jnp.float32) * validity[:, None, :], axis=2)

    blocks = child_schur.reshape(2, child_rowblk, BLK, child_colblk * BLK)
    section_one = []
    for k in range(2):
        outgoing = take_slabs(blocks[k], src_row[k]).reshape(row_slots * BLK, child_colblk * BLK)
        section_one.append(lax.all_to_all(outgoing, "row", split_axis=0, concat_axis=0, tiled=True))

    panel_width = PANEL // BLK
    corner_blk = jnp.arange(panel_width)
    col_hit = (jnp.take(child_index, local_bcol, axis=1)[:, None, :] == corner_blk[None, :, None])
    corner_cpick = jnp.sum(col_hit.astype(jnp.int32) * jnp.arange(child_colblk)[None, None, :], axis=2)
    corner_cw = jnp.sum(
        col_hit.astype(jnp.float32) * jnp.take(validity, local_bcol, axis=1)[:, None, :], axis=2
    )
    own = jnp.where(col_place < panel_width, front_matrix[:BLK, :BLK], jnp.zeros((BLK, BLK), jnp.float32))
    partial = lax.dynamic_update_slice(
        jnp.zeros((BLK, PANEL), jnp.float32), own, (0, jnp.minimum(col_place, panel_width - 1) * BLK)
    )
    for k in range(2):
        slab = lax.dynamic_slice_in_dim(section_one[k], row_source[k, 0] * BLK, BLK, axis=0)
        slab = (slab * row_weight[k, 0]).reshape(BLK, child_colblk, BLK)
        picked_cols = jnp.take(slab, corner_cpick[k], axis=1) * corner_cw[k][None, :, None]
        partial = partial + picked_cols.reshape(BLK, PANEL)
    corner_row = jnp.sum(lax.all_gather(partial, "col", axis=0, tiled=False), axis=0)
    corner = lax.all_gather(corner_row, "row", axis=0, tiled=True)

    arrived = []
    for k in range(2):
        flipped = section_one[k].T.reshape(child_colblk, BLK, row_slots * BLK)
        onward = take_slabs(flipped, src_col[k]) * has_col[k][:, None, None]
        onward = onward.reshape(col_slots * BLK, row_slots * BLK)
        if k == 0:
            lower_factor, inverse = factor_and_invert(corner)
        section_two = lax.all_to_all(onward, "col", split_axis=0, concat_axis=0, tiled=True)
        if k == 1:
            section_two, lower_factor, inverse = lax.optimization_barrier(
                (section_two, lower_factor, inverse)
            )
        arrived.append(section_two.reshape(col_slots, BLK, row_slots * BLK))
    arrived = jnp.stack(arrived)

    by_col = jax.vmap(take_slabs)(arrived, col_source) * col_weight[:, :, None, None]
    by_col = by_col.reshape(2, local_cols, row_slots * BLK)
    unflipped = jnp.swapaxes(by_col, 1, 2).reshape(2, row_slots, BLK, local_cols)
    placed = jax.vmap(take_slabs)(unflipped, row_source) * row_weight[:, :, None, None]
    placed = placed.reshape(2, local_rows, local_cols)
    extended = front_matrix + placed[0] + placed[1]

    spread = col_count // panel_width
    lead = front_matrix[:, :BLK]
    for k in range(2):
        first_col = lax.dynamic_index_in_dim(arrived[k], col_source[k, 0], axis=0, keepdims=False)
        first_col = (first_col * col_weight[k, 0]).T.reshape(row_slots, BLK, BLK)
        lead = lead + (take_slabs(first_col, row_source[k]) * row_weight[k][:, None, None]).reshape(
            local_rows, BLK
        )
    lifted = lax.ppermute(
        lead, "col", [(c, c + panel_width * s) for s in range(1, spread) for c in range(panel_width)]
    )
    mine = jnp.where(col_place < panel_width, lead, lifted)
    part_rows = local_rows // spread
    part = lax.dynamic_slice_in_dim(mine, (col_place // panel_width) * part_rows, part_rows, axis=0)
    part = part.reshape(part_rows * BLK // 128, 128)
    gathered = lax.all_gather(part, "col", axis=0, tiled=False)
    gathered, extended = lax.optimization_barrier((gathered, extended))
    gathered = gathered.reshape(spread, panel_width, part_rows, BLK)
    panel_cols = gathered.transpose(0, 2, 1, 3).reshape(local_rows, PANEL)

    solved = jnp.einsum("rp,qp->rq", panel_cols, inverse, precision=exact_mode)
    logical_blk = jnp.arange(row_blocks) * row_count + row_place
    factor_blocks = lower_factor.reshape(panel_width, BLK, PANEL)
    picked = jnp.take(factor_blocks, jnp.minimum(logical_blk, panel_width - 1), axis=0)
    in_panel = (logical_blk < panel_width)[:, None, None]
    panel_factor = jnp.where(in_panel, picked, solved.reshape(row_blocks, BLK, PANEL)).reshape(
        local_rows, PANEL
    )

    ratio = col_count // row_count
    arranged = panel_factor.reshape(col_blocks, ratio, BLK, PANEL)
    chosen = lax.dynamic_index_in_dim(arranged, col_place // row_count, axis=1, keepdims=False)
    chosen = chosen.reshape(col_blocks * BLK, PANEL)
    pairs = []
    for r0 in range(row_count):
        for c1 in range(col_count):
            dest_row = c1 % row_count
            dest_col = r0 + row_count * (c1 // row_count)
            pairs.append((r0 * col_count + c1, dest_row * col_count + dest_col))
    piece_rows = chosen.shape[0] // row_count
    piece = lax.dynamic_slice_in_dim(chosen, (col_place % row_count) * piece_rows, piece_rows, axis=0)
    piece = lax.ppermute(piece, ("row", "col"), pairs)
    across = lax.all_gather(piece, "row", axis=0, tiled=True)
    update = jnp.einsum("rp,cp->rc", panel_factor, across, precision=exact_mode)
    logical_row = jnp.arange(local_rows) // BLK * row_count + row_place
    logical_col = jnp.arange(local_cols) // BLK * col_count + col_place
    retained = (logical_row >= panel_width)[:, None] & (logical_col >= panel_width)[None, :]
    trailing = jnp.where(retained, extended - update, jnp.zeros_like(update))
    return (trailing, panel_factor)


def solution(mesh):
    in_specs = (P("row", "col"), P(None, "row", "col"), P(), P())
    out_specs = (P("row", "col"), P("row", None))
    return jax.shard_map(
        on_device, mesh=mesh, in_specs=in_specs, out_specs=out_specs, check_vma=False
    )
```

```python
import jax
import jax.numpy as jnp
from jax import lax
from jax.sharding import PartitionSpec as P

CHILD = 8192
PANEL = 512
BLK = 64


exact_mode = lax.Precision.HIGHEST


def take_slabs(source, indices):
    return jnp.take(source, indices, axis=0)


def factor_and_invert(corner, width=128):
    count = corner.shape[0] // width
    sym = (corner + corner.T) / 2
    grid = [[sym[i * width : (i + 1) * width, j * width : (j + 1) * width] for j in range(count)] for i in range(count)]
    eye = jnp.eye(width, dtype=corner.dtype)
    low = [[None] * count for _ in range(count)]
    diag_inv = []
    for p in range(count):
        lpp = lax.linalg.cholesky(grid[p][p], symmetrize_input=False)
        dinv = jax.scipy.linalg.solve_triangular(lpp, eye, lower=True)
        low[p][p] = lpp
        diag_inv.append(dinv)
        for i in range(p + 1, count):
            low[i][p] = jnp.dot(grid[i][p], dinv.T, precision=exact_mode)
        for i in range(p + 1, count):
            for j in range(p + 1, i + 1):
                grid[i][j] = grid[i][j] - jnp.dot(low[i][p], low[j][p].T, precision=exact_mode)
    zero = jnp.zeros((width, width), corner.dtype)
    inv = [[zero] * count for _ in range(count)]
    for j in range(count):
        inv[j][j] = diag_inv[j]
        for i in range(j + 1, count):
            acc = jnp.dot(low[i][j], inv[j][j], precision=exact_mode)
            for k in range(j + 1, i):
                acc = acc + jnp.dot(low[i][k], inv[k][j], precision=exact_mode)
            inv[i][j] = -jnp.dot(diag_inv[i], acc, precision=exact_mode)
    lower = jnp.block([[low[i][j] if j <= i else zero for j in range(count)] for i in range(count)])
    inverse = jnp.block(inv)
    return lower, inverse


def on_device(front_matrix, child_schur, child_index, child_valid):
    row_count = lax.axis_size("row")
    col_count = lax.axis_size("col")
    row_place = lax.axis_index("row")
    col_place = lax.axis_index("col")
    local_rows, local_cols = front_matrix.shape
    row_blocks = local_rows // BLK
    col_blocks = local_cols // BLK
    child_blocks = CHILD // BLK
    child_rowblk = child_schur.shape[1] // BLK
    child_colblk = child_schur.shape[2] // BLK
    per_owner = child_blocks // (row_count * row_count)
    col_multi = max(1, child_blocks // (col_count * col_count))
    row_slots = row_count * per_owner
    col_slots = col_count * col_multi
    validity = child_valid.astype(jnp.float32)
    all_blocks = jnp.arange(child_blocks)
    owner_row = child_index % row_count
    owner_col = child_index % col_count
    sender_row = all_blocks % row_count
    sender_col = all_blocks % col_count
    before = all_blocks[None, :] < all_blocks[:, None]
    earlier_row = (sender_row[:, None] == sender_row[None, :]) & before
    earlier_col = (sender_col[:, None] == sender_col[None, :]) & before
    row_rank = jnp.sum(
        (earlier_row[None] & (owner_row[:, :, None] == owner_row[:, None, :])).astype(jnp.int32),
        axis=2,
    )
    col_rank = jnp.sum(
        (earlier_col[None] & (owner_col[:, :, None] == owner_col[:, None, :])).astype(jnp.int32),
        axis=2,
    )
    row_key = owner_row * per_owner + row_rank
    col_key = owner_col * col_multi + col_rank
    local_arow = row_place + row_count * jnp.arange(child_rowblk)
    mine_rowkey = jnp.take(row_key, local_arow, axis=1)
    row_hit_send = mine_rowkey[:, :, None] == jnp.arange(row_slots)[None, None, :]
    src_row = jnp.sum(
        row_hit_send.astype(jnp.int32) * jnp.arange(child_rowblk)[None, :, None], axis=1
    )
    local_bcol = col_place + col_count * jnp.arange(child_colblk)
    mine_colkey = jnp.take(col_key, local_bcol, axis=1)
    col_hit_send = mine_colkey[:, :, None] == jnp.arange(col_slots)[None, None, :]
    src_col = jnp.sum(
        col_hit_send.astype(jnp.int32) * jnp.arange(child_colblk)[None, :, None], axis=1
    )
    has_col = jnp.sum(col_hit_send.astype(jnp.float32), axis=1)

    front_rowblk = row_place + row_count * jnp.arange(row_blocks)
    match_rows = (child_index[:, None, :] == front_rowblk[None, :, None]).astype(jnp.int32)
    row_slot_of = sender_row[None, :] * per_owner + row_rank
    row_source = jnp.sum(match_rows * row_slot_of[:, None, :], axis=2)
    row_weight = jnp.sum(match_rows.astype(jnp.float32) * validity[:, None, :], axis=2)
    front_colblk = col_place + col_count * jnp.arange(col_blocks)
    match_cols = (child_index[:, None, :] == front_colblk[None, :, None]).astype(jnp.int32)
    col_slot_of = sender_col[None, :] * col_multi + col_rank
    col_source = jnp.sum(match_cols * col_slot_of[:, None, :], axis=2)
    col_weight = jnp.sum(match_cols.astype(jnp.float32) * validity[:, None, :], axis=2)

    blocks = child_schur.reshape(2, child_rowblk, BLK, child_colblk * BLK)
    section_one = []
    for k in range(2):
        outgoing = take_slabs(blocks[k], src_row[k]).reshape(row_slots * BLK, child_colblk * BLK)
        section_one.append(lax.all_to_all(outgoing, "row", split_axis=0, concat_axis=0, tiled=True))

    panel_width = PANEL // BLK
    corner_blk = jnp.arange(panel_width)
    col_hit = (jnp.take(child_index, local_bcol, axis=1)[:, None, :] == corner_blk[None, :, None])
    corner_cpick = jnp.sum(col_hit.astype(jnp.int32) * jnp.arange(child_colblk)[None, None, :], axis=2)
    corner_cw = jnp.sum(
        col_hit.astype(jnp.float32) * jnp.take(validity, local_bcol, axis=1)[:, None, :], axis=2
    )
    own = jnp.where(col_place < panel_width, front_matrix[:BLK, :BLK], jnp.zeros((BLK, BLK), jnp.float32))
    partial = lax.dynamic_update_slice(
        jnp.zeros((BLK, PANEL), jnp.float32), own, (0, jnp.minimum(col_place, panel_width - 1) * BLK)
    )
    for k in range(2):
        slab = lax.dynamic_slice_in_dim(section_one[k], row_source[k, 0] * BLK, BLK, axis=0)
        slab = (slab * row_weight[k, 0]).reshape(BLK, child_colblk, BLK)
        picked_cols = jnp.take(slab, corner_cpick[k], axis=1) * corner_cw[k][None, :, None]
        partial = partial + picked_cols.reshape(BLK, PANEL)
    share = partial.reshape(col_count, BLK // col_count, PANEL)
    share = lax.all_to_all(share, "col", split_axis=0, concat_axis=0, tiled=True)
    share = jnp.sum(share, axis=0)
    corner_row = lax.all_gather(share, "col", axis=0, tiled=True)
    corner = lax.all_gather(corner_row, "row", axis=0, tiled=True)

    arrived = []
    for k in range(2):
        flipped = section_one[k].T.reshape(child_colblk, BLK, row_slots * BLK)
        onward = take_slabs(flipped, src_col[k]) * has_col[k][:, None, None]
        onward = onward.reshape(col_slots * BLK, row_slots * BLK)
        if k == 0:
            lower_factor, inverse = factor_and_invert(corner)
        section_two = lax.all_to_all(onward, "col", split_axis=0, concat_axis=0, tiled=True)
        if k == 1:
            section_two, lower_factor, inverse = lax.optimization_barrier(
                (section_two, lower_factor, inverse)
            )
        arrived.append(section_two.reshape(col_slots, BLK, row_slots * BLK))
    arrived = jnp.stack(arrived)

    by_col = jax.vmap(take_slabs)(arrived, col_source) * col_weight[:, :, None, None]
    by_col = by_col.reshape(2, local_cols, row_slots * BLK)
    unflipped = jnp.swapaxes(by_col, 1, 2).reshape(2, row_slots, BLK, local_cols)
    placed = jax.vmap(take_slabs)(unflipped, row_source) * row_weight[:, :, None, None]
    placed = placed.reshape(2, local_rows, local_cols)
    extended = front_matrix + placed[0] + placed[1]

    spread = col_count // panel_width
    lead = front_matrix[:, :BLK]
    for k in range(2):
        first_col = lax.dynamic_index_in_dim(arrived[k], col_source[k, 0], axis=0, keepdims=False)
        first_col = (first_col * col_weight[k, 0]).T.reshape(row_slots, BLK, BLK)
        lead = lead + (take_slabs(first_col, row_source[k]) * row_weight[k][:, None, None]).reshape(
            local_rows, BLK
        )
    lifted = lax.ppermute(
        lead, "col", [(c, c + panel_width * s) for s in range(1, spread) for c in range(panel_width)]
    )
    mine = jnp.where(col_place < panel_width, lead, lifted)
    part_rows = local_rows // spread
    part = lax.dynamic_slice_in_dim(mine, (col_place // panel_width) * part_rows, part_rows, axis=0)
    part = part.reshape(part_rows * BLK // 128, 128)
    gathered = lax.all_gather(part, "col", axis=0, tiled=False)
    gathered, extended = lax.optimization_barrier((gathered, extended))
    gathered = gathered.reshape(spread, panel_width, part_rows, BLK)
    panel_cols = gathered.transpose(0, 2, 1, 3).reshape(local_rows, PANEL)

    solved = jnp.einsum("rp,qp->rq", panel_cols, inverse, precision=exact_mode)
    logical_blk = jnp.arange(row_blocks) * row_count + row_place
    factor_blocks = lower_factor.reshape(panel_width, BLK, PANEL)
    picked = jnp.take(factor_blocks, jnp.minimum(logical_blk, panel_width - 1), axis=0)
    in_panel = (logical_blk < panel_width)[:, None, None]
    panel_factor = jnp.where(in_panel, picked, solved.reshape(row_blocks, BLK, PANEL)).reshape(
        local_rows, PANEL
    )

    ratio = col_count // row_count
    arranged = panel_factor.reshape(col_blocks, ratio, BLK, PANEL)
    chosen = lax.dynamic_index_in_dim(arranged, col_place // row_count, axis=1, keepdims=False)
    chosen = chosen.reshape(col_blocks * BLK, PANEL)
    pairs = []
    for r0 in range(row_count):
        for c1 in range(col_count):
            dest_row = c1 % row_count
            dest_col = r0 + row_count * (c1 // row_count)
            pairs.append((r0 * col_count + c1, dest_row * col_count + dest_col))
    piece_rows = chosen.shape[0] // row_count
    piece = lax.dynamic_slice_in_dim(chosen, (col_place % row_count) * piece_rows, piece_rows, axis=0)
    piece = lax.ppermute(piece, ("row", "col"), pairs)
    across = lax.all_gather(piece, "row", axis=0, tiled=True)
    update = jnp.einsum("rp,cp->rc", panel_factor, across, precision=exact_mode)
    logical_row = jnp.arange(local_rows) // BLK * row_count + row_place
    logical_col = jnp.arange(local_cols) // BLK * col_count + col_place
    retained = (logical_row >= panel_width)[:, None] & (logical_col >= panel_width)[None, :]
    trailing = jnp.where(retained, extended - update, jnp.zeros_like(update))
    return (trailing, panel_factor)


def solution(mesh):
    in_specs = (P("row", "col"), P(None, "row", "col"), P(), P())
    out_specs = (P("row", "col"), P("row", None))
    return jax.shard_map(
        on_device, mesh=mesh, in_specs=in_specs, out_specs=out_specs, check_vma=False
    )
```

```python
import jax
import jax.numpy as jnp
from jax import lax
from jax.sharding import PartitionSpec as P

CHILD = 8192
PANEL = 512
BLK = 64


exact_mode = lax.Precision.HIGHEST


def take_slabs(source, indices):
    return jnp.take(source, indices, axis=0)


def factor_and_invert(corner, width=128):
    count = corner.shape[0] // width
    sym = (corner + corner.T) / 2
    grid = [[sym[i * width : (i + 1) * width, j * width : (j + 1) * width] for j in range(count)] for i in range(count)]
    eye = jnp.eye(width, dtype=corner.dtype)
    low = [[None] * count for _ in range(count)]
    diag_inv = []
    for p in range(count):
        lpp = lax.linalg.cholesky(grid[p][p], symmetrize_input=False)
        dinv = jax.scipy.linalg.solve_triangular(lpp, eye, lower=True)
        low[p][p] = lpp
        diag_inv.append(dinv)
        for i in range(p + 1, count):
            low[i][p] = jnp.dot(grid[i][p], dinv.T, precision=exact_mode)
        for i in range(p + 1, count):
            for j in range(p + 1, i + 1):
                grid[i][j] = grid[i][j] - jnp.dot(low[i][p], low[j][p].T, precision=exact_mode)
    zero = jnp.zeros((width, width), corner.dtype)
    inv = [[zero] * count for _ in range(count)]
    for j in range(count):
        inv[j][j] = diag_inv[j]
        for i in range(j + 1, count):
            acc = jnp.dot(low[i][j], inv[j][j], precision=exact_mode)
            for k in range(j + 1, i):
                acc = acc + jnp.dot(low[i][k], inv[k][j], precision=exact_mode)
            inv[i][j] = -jnp.dot(diag_inv[i], acc, precision=exact_mode)
    lower = jnp.block([[low[i][j] if j <= i else zero for j in range(count)] for i in range(count)])
    inverse = jnp.block(inv)
    return lower, inverse


def on_device(front_matrix, child_schur, child_index, child_valid):
    row_count = lax.axis_size("row")
    col_count = lax.axis_size("col")
    row_place = lax.axis_index("row")
    col_place = lax.axis_index("col")
    local_rows, local_cols = front_matrix.shape
    row_blocks = local_rows // BLK
    col_blocks = local_cols // BLK
    child_blocks = CHILD // BLK
    child_rowblk = child_schur.shape[1] // BLK
    child_colblk = child_schur.shape[2] // BLK
    per_owner = child_blocks // (row_count * row_count)
    col_multi = max(1, child_blocks // (col_count * col_count))
    row_slots = row_count * per_owner
    col_slots = col_count * col_multi
    validity = child_valid.astype(jnp.float32)
    all_blocks = jnp.arange(child_blocks)
    owner_row = child_index % row_count
    owner_col = child_index % col_count
    sender_row = all_blocks % row_count
    sender_col = all_blocks % col_count
    before = all_blocks[None, :] < all_blocks[:, None]
    earlier_row = (sender_row[:, None] == sender_row[None, :]) & before
    earlier_col = (sender_col[:, None] == sender_col[None, :]) & before
    row_rank = jnp.sum(
        (earlier_row[None] & (owner_row[:, :, None] == owner_row[:, None, :])).astype(jnp.int32),
        axis=2,
    )
    col_rank = jnp.sum(
        (earlier_col[None] & (owner_col[:, :, None] == owner_col[:, None, :])).astype(jnp.int32),
        axis=2,
    )
    row_key = owner_row * per_owner + row_rank
    col_key = owner_col * col_multi + col_rank
    local_arow = row_place + row_count * jnp.arange(child_rowblk)
    mine_rowkey = jnp.take(row_key, local_arow, axis=1)
    row_hit_send = mine_rowkey[:, :, None] == jnp.arange(row_slots)[None, None, :]
    src_row = jnp.sum(
        row_hit_send.astype(jnp.int32) * jnp.arange(child_rowblk)[None, :, None], axis=1
    )
    local_bcol = col_place + col_count * jnp.arange(child_colblk)
    mine_colkey = jnp.take(col_key, local_bcol, axis=1)
    col_hit_send = mine_colkey[:, :, None] == jnp.arange(col_slots)[None, None, :]
    src_col = jnp.sum(
        col_hit_send.astype(jnp.int32) * jnp.arange(child_colblk)[None, :, None], axis=1
    )
    has_col = jnp.sum(col_hit_send.astype(jnp.float32), axis=1)

    front_rowblk = row_place + row_count * jnp.arange(row_blocks)
    match_rows = (child_index[:, None, :] == front_rowblk[None, :, None]).astype(jnp.int32)
    row_slot_of = sender_row[None, :] * per_owner + row_rank
    row_source = jnp.sum(match_rows * row_slot_of[:, None, :], axis=2)
    row_weight = jnp.sum(match_rows.astype(jnp.float32) * validity[:, None, :], axis=2)
    front_colblk = col_place + col_count * jnp.arange(col_blocks)
    match_cols = (child_index[:, None, :] == front_colblk[None, :, None]).astype(jnp.int32)
    col_slot_of = sender_col[None, :] * col_multi + col_rank
    col_source = jnp.sum(match_cols * col_slot_of[:, None, :], axis=2)
    col_weight = jnp.sum(match_cols.astype(jnp.float32) * validity[:, None, :], axis=2)

    blocks = child_schur.reshape(2, child_rowblk, BLK, child_colblk * BLK)
    section_one = []
    for k in range(2):
        outgoing = take_slabs(blocks[k], src_row[k]).reshape(row_slots * BLK, child_colblk * BLK)
        section_one.append(lax.all_to_all(outgoing, "row", split_axis=0, concat_axis=0, tiled=True))

    panel_width = PANEL // BLK
    corner_blk = jnp.arange(panel_width)
    col_hit = (jnp.take(child_index, local_bcol, axis=1)[:, None, :] == corner_blk[None, :, None])
    corner_cpick = jnp.sum(col_hit.astype(jnp.int32) * jnp.arange(child_colblk)[None, None, :], axis=2)
    corner_cw = jnp.sum(
        col_hit.astype(jnp.float32) * jnp.take(validity, local_bcol, axis=1)[:, None, :], axis=2
    )
    own = jnp.where(col_place < panel_width, front_matrix[:BLK, :BLK], jnp.zeros((BLK, BLK), jnp.float32))
    partial = lax.dynamic_update_slice(
        jnp.zeros((BLK, PANEL), jnp.float32), own, (0, jnp.minimum(col_place, panel_width - 1) * BLK)
    )
    for k in range(2):
        slab = lax.dynamic_slice_in_dim(section_one[k], row_source[k, 0] * BLK, BLK, axis=0)
        slab = (slab * row_weight[k, 0]).reshape(BLK, child_colblk, BLK)
        picked_cols = jnp.take(slab, corner_cpick[k], axis=1) * corner_cw[k][None, :, None]
        partial = partial + picked_cols.reshape(BLK, PANEL)
    share = partial.reshape(col_count, BLK // col_count, PANEL)
    share = lax.all_to_all(share, "col", split_axis=0, concat_axis=0, tiled=True)
    share = jnp.sum(share, axis=0)
    corner = lax.all_gather(share, ("row", "col"), axis=0, tiled=True)

    onward = []
    for k in range(2):
        flipped = section_one[k].T.reshape(child_colblk, BLK, row_slots * BLK)
        sent = take_slabs(flipped, src_col[k]) * has_col[k][:, None, None]
        onward.append(sent.reshape(col_slots * BLK, row_slots * BLK))
    onward = jnp.stack(onward)
    lower_factor, inverse = factor_and_invert(corner)
    section_two = lax.all_to_all(onward, "col", split_axis=1, concat_axis=1, tiled=True)
    section_two, lower_factor, inverse = lax.optimization_barrier((section_two, lower_factor, inverse))
    arrived = section_two.reshape(2, col_slots, BLK, row_slots * BLK)

    by_col = jax.vmap(take_slabs)(arrived, col_source) * col_weight[:, :, None, None]
    by_col = by_col.reshape(2, local_cols, row_slots * BLK)
    unflipped = jnp.swapaxes(by_col, 1, 2).reshape(2, row_slots, BLK, local_cols)
    placed = jax.vmap(take_slabs)(unflipped, row_source) * row_weight[:, :, None, None]
    placed = placed.reshape(2, local_rows, local_cols)
    extended = front_matrix + placed[0] + placed[1]

    spread = col_count // panel_width
    lead = front_matrix[:, :BLK]
    for k in range(2):
        first_col = lax.dynamic_index_in_dim(arrived[k], col_source[k, 0], axis=0, keepdims=False)
        first_col = (first_col * col_weight[k, 0]).T.reshape(row_slots, BLK, BLK)
        lead = lead + (take_slabs(first_col, row_source[k]) * row_weight[k][:, None, None]).reshape(
            local_rows, BLK
        )
    lifted = lax.ppermute(
        lead, "col", [(c, c + panel_width * s) for s in range(1, spread) for c in range(panel_width)]
    )
    mine = jnp.where(col_place < panel_width, lead, lifted)
    part_rows = local_rows // spread
    part = lax.dynamic_slice_in_dim(mine, (col_place // panel_width) * part_rows, part_rows, axis=0)
    part = part.reshape(part_rows * BLK // 128, 128)
    gathered = lax.all_gather(part, "col", axis=0, tiled=False)
    gathered, extended = lax.optimization_barrier((gathered, extended))
    gathered = gathered.reshape(spread, panel_width, part_rows, BLK)
    panel_cols = gathered.transpose(0, 2, 1, 3).reshape(local_rows, PANEL)

    solved = jnp.einsum("rp,qp->rq", panel_cols, inverse, precision=exact_mode)
    logical_blk = jnp.arange(row_blocks) * row_count + row_place
    factor_blocks = lower_factor.reshape(panel_width, BLK, PANEL)
    picked = jnp.take(factor_blocks, jnp.minimum(logical_blk, panel_width - 1), axis=0)
    in_panel = (logical_blk < panel_width)[:, None, None]
    panel_factor = jnp.where(in_panel, picked, solved.reshape(row_blocks, BLK, PANEL)).reshape(
        local_rows, PANEL
    )

    ratio = col_count // row_count
    arranged = panel_factor.reshape(col_blocks, ratio, BLK, PANEL)
    chosen = lax.dynamic_index_in_dim(arranged, col_place // row_count, axis=1, keepdims=False)
    chosen = chosen.reshape(col_blocks * BLK, PANEL)
    pairs = []
    for r0 in range(row_count):
        for c1 in range(col_count):
            dest_row = c1 % row_count
            dest_col = r0 + row_count * (c1 // row_count)
            pairs.append((r0 * col_count + c1, dest_row * col_count + dest_col))
    piece_rows = chosen.shape[0] // row_count
    piece = lax.dynamic_slice_in_dim(chosen, (col_place % row_count) * piece_rows, piece_rows, axis=0)
    piece = lax.ppermute(piece, ("row", "col"), pairs)
    across = lax.all_gather(piece, "row", axis=0, tiled=True)
    update = jnp.einsum("rp,cp->rc", panel_factor, across, precision=exact_mode)
    logical_row = jnp.arange(local_rows) // BLK * row_count + row_place
    logical_col = jnp.arange(local_cols) // BLK * col_count + col_place
    retained = (logical_row >= panel_width)[:, None] & (logical_col >= panel_width)[None, :]
    trailing = jnp.where(retained, extended - update, jnp.zeros_like(update))
    return (trailing, panel_factor)


def solution(mesh):
    in_specs = (P("row", "col"), P(None, "row", "col"), P(), P())
    out_specs = (P("row", "col"), P("row", None))
    return jax.shard_map(
        on_device, mesh=mesh, in_specs=in_specs, out_specs=out_specs, check_vma=False
    )
```

```python
import jax
import jax.numpy as jnp
from jax import lax
from jax.sharding import PartitionSpec as P

CHILD = 8192
PANEL = 512
BLK = 64


exact_mode = lax.Precision.HIGHEST


def take_slabs(source, indices):
    return jnp.take(source, indices, axis=0)


def factor_and_invert(corner, width=128):
    count = corner.shape[0] // width
    sym = (corner + corner.T) / 2
    grid = [[sym[i * width : (i + 1) * width, j * width : (j + 1) * width] for j in range(count)] for i in range(count)]
    eye = jnp.eye(width, dtype=corner.dtype)
    low = [[None] * count for _ in range(count)]
    diag_inv = []
    for p in range(count):
        lpp = lax.linalg.cholesky(grid[p][p], symmetrize_input=False)
        dinv = jax.scipy.linalg.solve_triangular(lpp, eye, lower=True)
        low[p][p] = lpp
        diag_inv.append(dinv)
        for i in range(p + 1, count):
            low[i][p] = jnp.dot(grid[i][p], dinv.T, precision=exact_mode)
        for i in range(p + 1, count):
            for j in range(p + 1, i + 1):
                grid[i][j] = grid[i][j] - jnp.dot(low[i][p], low[j][p].T, precision=exact_mode)
    zero = jnp.zeros((width, width), corner.dtype)
    inv = [[zero] * count for _ in range(count)]
    for j in range(count):
        inv[j][j] = diag_inv[j]
        for i in range(j + 1, count):
            acc = jnp.dot(low[i][j], inv[j][j], precision=exact_mode)
            for k in range(j + 1, i):
                acc = acc + jnp.dot(low[i][k], inv[k][j], precision=exact_mode)
            inv[i][j] = -jnp.dot(diag_inv[i], acc, precision=exact_mode)
    lower = jnp.block([[low[i][j] if j <= i else zero for j in range(count)] for i in range(count)])
    inverse = jnp.block(inv)
    return lower, inverse


def on_device(front_matrix, child_schur, child_index, child_valid):
    row_count = lax.axis_size("row")
    col_count = lax.axis_size("col")
    row_place = lax.axis_index("row")
    col_place = lax.axis_index("col")
    local_rows, local_cols = front_matrix.shape
    row_blocks = local_rows // BLK
    col_blocks = local_cols // BLK
    child_blocks = CHILD // BLK
    child_rowblk = child_schur.shape[1] // BLK
    child_colblk = child_schur.shape[2] // BLK
    per_owner = child_blocks // (row_count * row_count)
    col_multi = max(1, child_blocks // (col_count * col_count))
    row_slots = row_count * per_owner
    col_slots = col_count * col_multi
    validity = child_valid.astype(jnp.float32)
    all_blocks = jnp.arange(child_blocks)
    owner_row = child_index % row_count
    owner_col = child_index % col_count
    sender_row = all_blocks % row_count
    sender_col = all_blocks % col_count
    before = all_blocks[None, :] < all_blocks[:, None]
    earlier_row = (sender_row[:, None] == sender_row[None, :]) & before
    earlier_col = (sender_col[:, None] == sender_col[None, :]) & before
    row_rank = jnp.sum(
        (earlier_row[None] & (owner_row[:, :, None] == owner_row[:, None, :])).astype(jnp.int32),
        axis=2,
    )
    col_rank = jnp.sum(
        (earlier_col[None] & (owner_col[:, :, None] == owner_col[:, None, :])).astype(jnp.int32),
        axis=2,
    )
    row_key = owner_row * per_owner + row_rank
    col_key = owner_col * col_multi + col_rank
    local_arow = row_place + row_count * jnp.arange(child_rowblk)
    mine_rowkey = jnp.take(row_key, local_arow, axis=1)
    row_hit_send = mine_rowkey[:, :, None] == jnp.arange(row_slots)[None, None, :]
    src_row = jnp.sum(
        row_hit_send.astype(jnp.int32) * jnp.arange(child_rowblk)[None, :, None], axis=1
    )
    local_bcol = col_place + col_count * jnp.arange(child_colblk)
    mine_colkey = jnp.take(col_key, local_bcol, axis=1)
    col_hit_send = mine_colkey[:, :, None] == jnp.arange(col_slots)[None, None, :]
    src_col = jnp.sum(
        col_hit_send.astype(jnp.int32) * jnp.arange(child_colblk)[None, :, None], axis=1
    )
    has_col = jnp.sum(col_hit_send.astype(jnp.float32), axis=1)

    front_rowblk = row_place + row_count * jnp.arange(row_blocks)
    match_rows = (child_index[:, None, :] == front_rowblk[None, :, None]).astype(jnp.int32)
    row_slot_of = sender_row[None, :] * per_owner + row_rank
    row_source = jnp.sum(match_rows * row_slot_of[:, None, :], axis=2)
    row_weight = jnp.sum(match_rows.astype(jnp.float32) * validity[:, None, :], axis=2)
    front_colblk = col_place + col_count * jnp.arange(col_blocks)
    match_cols = (child_index[:, None, :] == front_colblk[None, :, None]).astype(jnp.int32)
    col_slot_of = sender_col[None, :] * col_multi + col_rank
    col_source = jnp.sum(match_cols * col_slot_of[:, None, :], axis=2)
    col_weight = jnp.sum(match_cols.astype(jnp.float32) * validity[:, None, :], axis=2)

    blocks = child_schur.reshape(2, child_rowblk, BLK, child_colblk * BLK)
    section_one = []
    for k in range(2):
        outgoing = take_slabs(blocks[k], src_row[k]).reshape(row_slots * BLK, child_colblk * BLK)
        section_one.append(lax.all_to_all(outgoing, "row", split_axis=0, concat_axis=0, tiled=True))

    panel_width = PANEL // BLK
    corner_blk = jnp.arange(panel_width)
    col_hit = (jnp.take(child_index, local_bcol, axis=1)[:, None, :] == corner_blk[None, :, None])
    corner_cpick = jnp.sum(col_hit.astype(jnp.int32) * jnp.arange(child_colblk)[None, None, :], axis=2)
    corner_cw = jnp.sum(
        col_hit.astype(jnp.float32) * jnp.take(validity, local_bcol, axis=1)[:, None, :], axis=2
    )
    own = jnp.where(col_place < panel_width, front_matrix[:BLK, :BLK], jnp.zeros((BLK, BLK), jnp.float32))
    partial = lax.dynamic_update_slice(
        jnp.zeros((BLK, PANEL), jnp.float32), own, (0, jnp.minimum(col_place, panel_width - 1) * BLK)
    )
    for k in range(2):
        slab = lax.dynamic_slice_in_dim(section_one[k], row_source[k, 0] * BLK, BLK, axis=0)
        slab = (slab * row_weight[k, 0]).reshape(BLK, child_colblk, BLK)
        picked_cols = jnp.take(slab, corner_cpick[k], axis=1) * corner_cw[k][None, :, None]
        partial = partial + picked_cols.reshape(BLK, PANEL)
    share = partial.reshape(col_count, BLK // col_count, PANEL)
    share = lax.all_to_all(share, "col", split_axis=0, concat_axis=0, tiled=True)
    share = jnp.sum(share, axis=0)
    corner_row = lax.all_gather(share, "col", axis=0, tiled=True)
    corner = lax.all_gather(corner_row, "row", axis=0, tiled=True)

    onward = []
    for k in range(2):
        flipped = section_one[k].T.reshape(child_colblk, BLK, row_slots * BLK)
        sent = take_slabs(flipped, src_col[k]) * has_col[k][:, None, None]
        onward.append(sent.reshape(col_slots * BLK, row_slots * BLK))
    onward = jnp.stack(onward)
    lower_factor, inverse = factor_and_invert(corner)
    section_two = lax.all_to_all(onward, "col", split_axis=1, concat_axis=1, tiled=True)
    section_two, lower_factor, inverse = lax.optimization_barrier((section_two, lower_factor, inverse))
    arrived = section_two.reshape(2, col_slots, BLK, row_slots * BLK)

    by_col = jax.vmap(take_slabs)(arrived, col_source) * col_weight[:, :, None, None]
    by_col = by_col.reshape(2, local_cols, row_slots * BLK)
    unflipped = jnp.swapaxes(by_col, 1, 2).reshape(2, row_slots, BLK, local_cols)
    placed = jax.vmap(take_slabs)(unflipped, row_source) * row_weight[:, :, None, None]
    placed = placed.reshape(2, local_rows, local_cols)
    extended = front_matrix + placed[0] + placed[1]

    spread = col_count // panel_width
    lead = front_matrix[:, :BLK]
    for k in range(2):
        first_col = lax.dynamic_index_in_dim(arrived[k], col_source[k, 0], axis=0, keepdims=False)
        first_col = (first_col * col_weight[k, 0]).T.reshape(row_slots, BLK, BLK)
        lead = lead + (take_slabs(first_col, row_source[k]) * row_weight[k][:, None, None]).reshape(
            local_rows, BLK
        )
    lifted = lax.ppermute(
        lead, "col", [(c, c + panel_width * s) for s in range(1, spread) for c in range(panel_width)]
    )
    mine = jnp.where(col_place < panel_width, lead, lifted)
    part_rows = local_rows // spread
    part = lax.dynamic_slice_in_dim(mine, (col_place // panel_width) * part_rows, part_rows, axis=0)
    part = part.reshape(part_rows * BLK // 128, 128)
    gathered = lax.all_gather(part, "col", axis=0, tiled=False)
    gathered, extended = lax.optimization_barrier((gathered, extended))
    gathered = gathered.reshape(spread, panel_width, part_rows, BLK)
    panel_cols = gathered.transpose(0, 2, 1, 3).reshape(local_rows, PANEL)

    solved = jnp.einsum("rp,qp->rq", panel_cols, inverse, precision=exact_mode)
    logical_blk = jnp.arange(row_blocks) * row_count + row_place
    factor_blocks = lower_factor.reshape(panel_width, BLK, PANEL)
    picked = jnp.take(factor_blocks, jnp.minimum(logical_blk, panel_width - 1), axis=0)
    in_panel = (logical_blk < panel_width)[:, None, None]
    panel_factor = jnp.where(in_panel, picked, solved.reshape(row_blocks, BLK, PANEL)).reshape(
        local_rows, PANEL
    )

    ratio = col_count // row_count
    arranged = panel_factor.reshape(col_blocks, ratio, BLK, PANEL)
    chosen = lax.dynamic_index_in_dim(arranged, col_place // row_count, axis=1, keepdims=False)
    chosen = chosen.reshape(col_blocks * BLK, PANEL)
    pairs = []
    for r0 in range(row_count):
        for c1 in range(col_count):
            dest_row = c1 % row_count
            dest_col = r0 + row_count * (c1 // row_count)
            pairs.append((r0 * col_count + c1, dest_row * col_count + dest_col))
    piece_rows = chosen.shape[0] // row_count
    piece = lax.dynamic_slice_in_dim(chosen, (col_place % row_count) * piece_rows, piece_rows, axis=0)
    piece = lax.ppermute(piece, ("row", "col"), pairs)
    across = lax.all_gather(piece, "row", axis=0, tiled=True)
    update = jnp.einsum("rp,cp->rc", panel_factor, across, precision=exact_mode)
    logical_row = jnp.arange(local_rows) // BLK * row_count + row_place
    logical_col = jnp.arange(local_cols) // BLK * col_count + col_place
    retained = (logical_row >= panel_width)[:, None] & (logical_col >= panel_width)[None, :]
    trailing = jnp.where(retained, extended - update, jnp.zeros_like(update))
    return (trailing, panel_factor)


def solution(mesh):
    in_specs = (P("row", "col"), P(None, "row", "col"), P(), P())
    out_specs = (P("row", "col"), P("row", None))
    return jax.shard_map(
        on_device, mesh=mesh, in_specs=in_specs, out_specs=out_specs, check_vma=False
    )
```

```python
import jax
import jax.numpy as jnp
from jax import lax
from jax.sharding import PartitionSpec as P

CHILD = 8192
PANEL = 512
BLK = 64


exact_mode = lax.Precision.HIGHEST


def take_slabs(source, indices):
    return jnp.take(source, indices, axis=0)


def factor_and_invert(corner, width=128):
    count = corner.shape[0] // width
    sym = (corner + corner.T) / 2
    grid = [[sym[i * width : (i + 1) * width, j * width : (j + 1) * width] for j in range(count)] for i in range(count)]
    eye = jnp.eye(width, dtype=corner.dtype)
    low = [[None] * count for _ in range(count)]
    diag_inv = []
    for p in range(count):
        lpp = lax.linalg.cholesky(grid[p][p], symmetrize_input=False)
        dinv = jax.scipy.linalg.solve_triangular(lpp, eye, lower=True)
        low[p][p] = lpp
        diag_inv.append(dinv)
        for i in range(p + 1, count):
            low[i][p] = jnp.dot(grid[i][p], dinv.T, precision=exact_mode)
        for i in range(p + 1, count):
            for j in range(p + 1, i + 1):
                grid[i][j] = grid[i][j] - jnp.dot(low[i][p], low[j][p].T, precision=exact_mode)
    zero = jnp.zeros((width, width), corner.dtype)
    inv = [[zero] * count for _ in range(count)]
    for j in range(count):
        inv[j][j] = diag_inv[j]
        for i in range(j + 1, count):
            acc = jnp.dot(low[i][j], inv[j][j], precision=exact_mode)
            for k in range(j + 1, i):
                acc = acc + jnp.dot(low[i][k], inv[k][j], precision=exact_mode)
            inv[i][j] = -jnp.dot(diag_inv[i], acc, precision=exact_mode)
    lower = jnp.block([[low[i][j] if j <= i else zero for j in range(count)] for i in range(count)])
    inverse = jnp.block(inv)
    return lower, inverse


def on_device(front_matrix, child_schur, child_index, child_valid):
    row_count = lax.axis_size("row")
    col_count = lax.axis_size("col")
    row_place = lax.axis_index("row")
    col_place = lax.axis_index("col")
    local_rows, local_cols = front_matrix.shape
    row_blocks = local_rows // BLK
    col_blocks = local_cols // BLK
    child_blocks = CHILD // BLK
    child_rowblk = child_schur.shape[1] // BLK
    child_colblk = child_schur.shape[2] // BLK
    per_owner = child_blocks // (row_count * row_count)
    col_multi = max(1, child_blocks // (col_count * col_count))
    row_slots = row_count * per_owner
    col_slots = col_count * col_multi
    validity = child_valid.astype(jnp.float32)
    all_blocks = jnp.arange(child_blocks)
    owner_row = child_index % row_count
    owner_col = child_index % col_count
    sender_row = all_blocks % row_count
    sender_col = all_blocks % col_count
    before = all_blocks[None, :] < all_blocks[:, None]
    earlier_row = (sender_row[:, None] == sender_row[None, :]) & before
    earlier_col = (sender_col[:, None] == sender_col[None, :]) & before
    row_rank = jnp.sum(
        (earlier_row[None] & (owner_row[:, :, None] == owner_row[:, None, :])).astype(jnp.int32),
        axis=2,
    )
    col_rank = jnp.sum(
        (earlier_col[None] & (owner_col[:, :, None] == owner_col[:, None, :])).astype(jnp.int32),
        axis=2,
    )
    row_key = owner_row * per_owner + row_rank
    col_key = owner_col * col_multi + col_rank
    local_arow = row_place + row_count * jnp.arange(child_rowblk)
    mine_rowkey = jnp.take(row_key, local_arow, axis=1)
    row_hit_send = mine_rowkey[:, :, None] == jnp.arange(row_slots)[None, None, :]
    src_row = jnp.sum(
        row_hit_send.astype(jnp.int32) * jnp.arange(child_rowblk)[None, :, None], axis=1
    )
    local_bcol = col_place + col_count * jnp.arange(child_colblk)
    mine_colkey = jnp.take(col_key, local_bcol, axis=1)
    col_hit_send = mine_colkey[:, :, None] == jnp.arange(col_slots)[None, None, :]
    src_col = jnp.sum(
        col_hit_send.astype(jnp.int32) * jnp.arange(child_colblk)[None, :, None], axis=1
    )
    has_col = jnp.sum(col_hit_send.astype(jnp.float32), axis=1)

    front_rowblk = row_place + row_count * jnp.arange(row_blocks)
    match_rows = (child_index[:, None, :] == front_rowblk[None, :, None]).astype(jnp.int32)
    row_slot_of = sender_row[None, :] * per_owner + row_rank
    row_source = jnp.sum(match_rows * row_slot_of[:, None, :], axis=2)
    row_weight = jnp.sum(match_rows.astype(jnp.float32) * validity[:, None, :], axis=2)
    front_colblk = col_place + col_count * jnp.arange(col_blocks)
    match_cols = (child_index[:, None, :] == front_colblk[None, :, None]).astype(jnp.int32)
    col_slot_of = sender_col[None, :] * col_multi + col_rank
    col_source = jnp.sum(match_cols * col_slot_of[:, None, :], axis=2)
    col_weight = jnp.sum(match_cols.astype(jnp.float32) * validity[:, None, :], axis=2)

    blocks = child_schur.reshape(2, child_rowblk, BLK, child_colblk * BLK)
    section_one = []
    for k in range(2):
        outgoing = take_slabs(blocks[k], src_row[k]).reshape(row_slots * BLK, child_colblk * BLK)
        section_one.append(lax.all_to_all(outgoing, "row", split_axis=0, concat_axis=0, tiled=True))

    panel_width = PANEL // BLK
    corner_blk = jnp.arange(panel_width)
    col_hit = (jnp.take(child_index, local_bcol, axis=1)[:, None, :] == corner_blk[None, :, None])
    corner_cpick = jnp.sum(col_hit.astype(jnp.int32) * jnp.arange(child_colblk)[None, None, :], axis=2)
    corner_cw = jnp.sum(
        col_hit.astype(jnp.float32) * jnp.take(validity, local_bcol, axis=1)[:, None, :], axis=2
    )
    own = jnp.where(col_place < panel_width, front_matrix[:BLK, :BLK], jnp.zeros((BLK, BLK), jnp.float32))
    partial = lax.dynamic_update_slice(
        jnp.zeros((BLK, PANEL), jnp.float32), own, (0, jnp.minimum(col_place, panel_width - 1) * BLK)
    )
    for k in range(2):
        slab = lax.dynamic_slice_in_dim(section_one[k], row_source[k, 0] * BLK, BLK, axis=0)
        slab = (slab * row_weight[k, 0]).reshape(BLK, child_colblk, BLK)
        picked_cols = jnp.take(slab, corner_cpick[k], axis=1) * corner_cw[k][None, :, None]
        partial = partial + picked_cols.reshape(BLK, PANEL)
    share = partial.reshape(col_count, BLK // col_count, PANEL)
    share = lax.all_to_all(share, "col", split_axis=0, concat_axis=0, tiled=True)
    share = jnp.sum(share, axis=0)
    corner_row = lax.all_gather(share, "col", axis=0, tiled=True)
    corner = lax.all_gather(corner_row, "row", axis=0, tiled=True)

    onward = []
    for k in range(2):
        flipped = section_one[k].T.reshape(child_colblk, BLK, row_slots * BLK)
        sent = take_slabs(flipped, src_col[k]) * has_col[k][:, None, None]
        onward.append(sent.reshape(col_slots * BLK, row_slots * BLK))
    onward = jnp.stack(onward)
    lower_factor, inverse = factor_and_invert(corner)
    section_two = lax.all_to_all(onward, "col", split_axis=1, concat_axis=1, tiled=True)
    section_two, lower_factor, inverse = lax.optimization_barrier((section_two, lower_factor, inverse))
    arrived = section_two.reshape(2, col_slots, BLK, row_slots * BLK)

    by_col = jax.vmap(take_slabs)(arrived, col_source) * col_weight[:, :, None, None]
    by_col = by_col.reshape(2, local_cols, row_slots * BLK)
    unflipped = jnp.swapaxes(by_col, 1, 2).reshape(2, row_slots, BLK, local_cols)
    placed = jax.vmap(take_slabs)(unflipped, row_source) * row_weight[:, :, None, None]
    placed = placed.reshape(2, local_rows, local_cols)
    extended = front_matrix + placed[0] + placed[1]

    spread = col_count // panel_width
    lead = front_matrix[:, :BLK]
    for k in range(2):
        first_col = lax.dynamic_index_in_dim(arrived[k], col_source[k, 0], axis=0, keepdims=False)
        first_col = (first_col * col_weight[k, 0]).T.reshape(row_slots, BLK, BLK)
        lead = lead + (take_slabs(first_col, row_source[k]) * row_weight[k][:, None, None]).reshape(
            local_rows, BLK
        )
    part_rows = local_rows // spread
    part = lead[:part_rows]
    for h in range(1, spread):
        moved = lax.ppermute(
            lead[h * part_rows : (h + 1) * part_rows],
            "col",
            [(c, c + panel_width * h) for c in range(panel_width)],
        )
        part = jnp.where(col_place // panel_width == h, moved, part)
    part = part.reshape(part_rows * BLK // 128, 128)
    gathered = lax.all_gather(part, "col", axis=0, tiled=False)
    gathered, extended = lax.optimization_barrier((gathered, extended))
    gathered = gathered.reshape(spread, panel_width, part_rows, BLK)
    panel_cols = gathered.transpose(0, 2, 1, 3).reshape(local_rows, PANEL)

    solved = jnp.einsum("rp,qp->rq", panel_cols, inverse, precision=exact_mode)
    logical_blk = jnp.arange(row_blocks) * row_count + row_place
    factor_blocks = lower_factor.reshape(panel_width, BLK, PANEL)
    picked = jnp.take(factor_blocks, jnp.minimum(logical_blk, panel_width - 1), axis=0)
    in_panel = (logical_blk < panel_width)[:, None, None]
    panel_factor = jnp.where(in_panel, picked, solved.reshape(row_blocks, BLK, PANEL)).reshape(
        local_rows, PANEL
    )

    ratio = col_count // row_count
    arranged = panel_factor.reshape(col_blocks, ratio, BLK, PANEL)
    chosen = lax.dynamic_index_in_dim(arranged, col_place // row_count, axis=1, keepdims=False)
    chosen = chosen.reshape(col_blocks * BLK, PANEL)
    pairs = []
    for r0 in range(row_count):
        for c1 in range(col_count):
            dest_row = c1 % row_count
            dest_col = r0 + row_count * (c1 // row_count)
            pairs.append((r0 * col_count + c1, dest_row * col_count + dest_col))
    piece_rows = chosen.shape[0] // row_count
    piece = lax.dynamic_slice_in_dim(chosen, (col_place % row_count) * piece_rows, piece_rows, axis=0)
    piece = lax.ppermute(piece, ("row", "col"), pairs)
    across = lax.all_gather(piece, "row", axis=0, tiled=True)
    update = jnp.einsum("rp,cp->rc", panel_factor, across, precision=exact_mode)
    logical_row = jnp.arange(local_rows) // BLK * row_count + row_place
    logical_col = jnp.arange(local_cols) // BLK * col_count + col_place
    retained = (logical_row >= panel_width)[:, None] & (logical_col >= panel_width)[None, :]
    trailing = jnp.where(retained, extended - update, jnp.zeros_like(update))
    return (trailing, panel_factor)


def solution(mesh):
    in_specs = (P("row", "col"), P(None, "row", "col"), P(), P())
    out_specs = (P("row", "col"), P("row", None))
    return jax.shard_map(
        on_device, mesh=mesh, in_specs=in_specs, out_specs=out_specs, check_vma=False
    )
```

```python
import jax
import jax.numpy as jnp
from jax import lax
from jax.sharding import PartitionSpec as P

CHILD = 8192
PANEL = 512
BLK = 64


exact_mode = lax.Precision.HIGHEST


def take_slabs(source, indices):
    return jnp.take(source, indices, axis=0)


def factor_and_invert(corner, width=128):
    count = corner.shape[0] // width
    sym = (corner + corner.T) / 2
    grid = [[sym[i * width : (i + 1) * width, j * width : (j + 1) * width] for j in range(count)] for i in range(count)]
    eye = jnp.eye(width, dtype=corner.dtype)
    low = [[None] * count for _ in range(count)]
    diag_inv = []
    for p in range(count):
        lpp = lax.linalg.cholesky(grid[p][p], symmetrize_input=False)
        dinv = jax.scipy.linalg.solve_triangular(lpp, eye, lower=True)
        low[p][p] = lpp
        diag_inv.append(dinv)
        for i in range(p + 1, count):
            low[i][p] = jnp.dot(grid[i][p], dinv.T, precision=exact_mode)
        for i in range(p + 1, count):
            for j in range(p + 1, i + 1):
                grid[i][j] = grid[i][j] - jnp.dot(low[i][p], low[j][p].T, precision=exact_mode)
    zero = jnp.zeros((width, width), corner.dtype)
    inv = [[zero] * count for _ in range(count)]
    for j in range(count):
        inv[j][j] = diag_inv[j]
        for i in range(j + 1, count):
            acc = jnp.dot(low[i][j], inv[j][j], precision=exact_mode)
            for k in range(j + 1, i):
                acc = acc + jnp.dot(low[i][k], inv[k][j], precision=exact_mode)
            inv[i][j] = -jnp.dot(diag_inv[i], acc, precision=exact_mode)
    lower = jnp.block([[low[i][j] if j <= i else zero for j in range(count)] for i in range(count)])
    inverse = jnp.block(inv)
    return lower, inverse


def on_device(front_matrix, child_schur, child_index, child_valid):
    row_count = lax.axis_size("row")
    col_count = lax.axis_size("col")
    row_place = lax.axis_index("row")
    col_place = lax.axis_index("col")
    local_rows, local_cols = front_matrix.shape
    row_blocks = local_rows // BLK
    col_blocks = local_cols // BLK
    child_blocks = CHILD // BLK
    child_rowblk = child_schur.shape[1] // BLK
    child_colblk = child_schur.shape[2] // BLK
    per_owner = child_blocks // (row_count * row_count)
    col_multi = max(1, child_blocks // (col_count * col_count))
    row_slots = row_count * per_owner
    col_slots = col_count * col_multi
    validity = child_valid.astype(jnp.float32)
    all_blocks = jnp.arange(child_blocks)
    owner_row = child_index % row_count
    owner_col = child_index % col_count
    sender_row = all_blocks % row_count
    sender_col = all_blocks % col_count
    before = all_blocks[None, :] < all_blocks[:, None]
    earlier_row = (sender_row[:, None] == sender_row[None, :]) & before
    earlier_col = (sender_col[:, None] == sender_col[None, :]) & before
    row_rank = jnp.sum(
        (earlier_row[None] & (owner_row[:, :, None] == owner_row[:, None, :])).astype(jnp.int32),
        axis=2,
    )
    col_rank = jnp.sum(
        (earlier_col[None] & (owner_col[:, :, None] == owner_col[:, None, :])).astype(jnp.int32),
        axis=2,
    )
    row_key = owner_row * per_owner + row_rank
    col_key = owner_col * col_multi + col_rank
    local_arow = row_place + row_count * jnp.arange(child_rowblk)
    mine_rowkey = jnp.take(row_key, local_arow, axis=1)
    row_hit_send = mine_rowkey[:, :, None] == jnp.arange(row_slots)[None, None, :]
    src_row = jnp.sum(
        row_hit_send.astype(jnp.int32) * jnp.arange(child_rowblk)[None, :, None], axis=1
    )
    local_bcol = col_place + col_count * jnp.arange(child_colblk)
    mine_colkey = jnp.take(col_key, local_bcol, axis=1)
    col_hit_send = mine_colkey[:, :, None] == jnp.arange(col_slots)[None, None, :]
    src_col = jnp.sum(
        col_hit_send.astype(jnp.int32) * jnp.arange(child_colblk)[None, :, None], axis=1
    )
    has_col = jnp.sum(col_hit_send.astype(jnp.float32), axis=1)

    front_rowblk = row_place + row_count * jnp.arange(row_blocks)
    match_rows = (child_index[:, None, :] == front_rowblk[None, :, None]).astype(jnp.int32)
    row_slot_of = sender_row[None, :] * per_owner + row_rank
    row_source = jnp.sum(match_rows * row_slot_of[:, None, :], axis=2)
    row_weight = jnp.sum(match_rows.astype(jnp.float32) * validity[:, None, :], axis=2)
    front_colblk = col_place + col_count * jnp.arange(col_blocks)
    match_cols = (child_index[:, None, :] == front_colblk[None, :, None]).astype(jnp.int32)
    col_slot_of = sender_col[None, :] * col_multi + col_rank
    col_source = jnp.sum(match_cols * col_slot_of[:, None, :], axis=2)
    col_weight = jnp.sum(match_cols.astype(jnp.float32) * validity[:, None, :], axis=2)

    blocks = child_schur.reshape(2, child_rowblk, BLK, child_colblk * BLK)
    section_one = []
    for k in range(2):
        outgoing = take_slabs(blocks[k], src_row[k]).reshape(row_slots * BLK, child_colblk * BLK)
        section_one.append(lax.all_to_all(outgoing, "row", split_axis=0, concat_axis=0, tiled=True))

    panel_width = PANEL // BLK
    corner_blk = jnp.arange(panel_width)
    col_hit = (jnp.take(child_index, local_bcol, axis=1)[:, None, :] == corner_blk[None, :, None])
    corner_cpick = jnp.sum(col_hit.astype(jnp.int32) * jnp.arange(child_colblk)[None, None, :], axis=2)
    corner_cw = jnp.sum(
        col_hit.astype(jnp.float32) * jnp.take(validity, local_bcol, axis=1)[:, None, :], axis=2
    )
    own = jnp.where(col_place < panel_width, front_matrix[:BLK, :BLK], jnp.zeros((BLK, BLK), jnp.float32))
    partial = lax.dynamic_update_slice(
        jnp.zeros((BLK, PANEL), jnp.float32), own, (0, jnp.minimum(col_place, panel_width - 1) * BLK)
    )
    for k in range(2):
        slab = lax.dynamic_slice_in_dim(section_one[k], row_source[k, 0] * BLK, BLK, axis=0)
        slab = (slab * row_weight[k, 0]).reshape(BLK, child_colblk, BLK)
        picked_cols = jnp.take(slab, corner_cpick[k], axis=1) * corner_cw[k][None, :, None]
        partial = partial + picked_cols.reshape(BLK, PANEL)
    share = partial.reshape(col_count, BLK // col_count, PANEL)
    share = lax.all_to_all(share, "col", split_axis=0, concat_axis=0, tiled=True)
    share = jnp.sum(share, axis=0)
    corner_row = lax.all_gather(share, "col", axis=0, tiled=True)
    corner = lax.all_gather(corner_row, "row", axis=0, tiled=True)

    onward = []
    for k in range(2):
        flipped = section_one[k].T.reshape(child_colblk, BLK, row_slots * BLK)
        sent = take_slabs(flipped, src_col[k]) * has_col[k][:, None, None]
        onward.append(sent.reshape(col_slots * BLK, row_slots * BLK))
    onward = jnp.stack(onward)
    lower_factor, inverse = factor_and_invert(corner)
    section_two = lax.all_to_all(onward, "col", split_axis=1, concat_axis=1, tiled=True)
    section_two, lower_factor, inverse = lax.optimization_barrier((section_two, lower_factor, inverse))
    arrived = section_two.reshape(2, col_slots, BLK, row_slots * BLK)

    by_col = jax.vmap(take_slabs)(arrived, col_source) * col_weight[:, :, None, None]
    by_col = by_col.reshape(2, local_cols, row_slots * BLK)
    unflipped = jnp.swapaxes(by_col, 1, 2).reshape(2, row_slots, BLK, local_cols)
    placed = jax.vmap(take_slabs)(unflipped, row_source) * row_weight[:, :, None, None]
    placed = placed.reshape(2, local_rows, local_cols)
    extended = front_matrix + placed[0] + placed[1]

    spread = col_count // panel_width
    lead = front_matrix[:, :BLK]
    for k in range(2):
        first_col = lax.dynamic_index_in_dim(arrived[k], col_source[k, 0], axis=0, keepdims=False)
        first_col = (first_col * col_weight[k, 0]).T.reshape(row_slots, BLK, BLK)
        lead = lead + (take_slabs(first_col, row_source[k]) * row_weight[k][:, None, None]).reshape(
            local_rows, BLK
        )
    part_rows = local_rows // spread
    part = lead[:part_rows]
    for h in range(1, spread):
        moved = lax.ppermute(
            lead[h * part_rows : (h + 1) * part_rows],
            "col",
            [(c, c + panel_width * h) for c in range(panel_width)],
        )
        part = jnp.where(col_place // panel_width == h, moved, part)
    part = part.reshape(part_rows * BLK // 128, 128)
    gathered = lax.all_gather(part, "col", axis=0, tiled=False)
    gathered, extended = lax.optimization_barrier((gathered, extended))
    gathered = gathered.reshape(spread, panel_width, part_rows, BLK)
    panel_cols = gathered.transpose(0, 2, 1, 3).reshape(local_rows, PANEL)

    solved = jnp.einsum("rp,qp->rq", panel_cols, inverse, precision=exact_mode)
    logical_blk = jnp.arange(row_blocks) * row_count + row_place
    factor_blocks = lower_factor.reshape(panel_width, BLK, PANEL)
    picked = jnp.take(factor_blocks, jnp.minimum(logical_blk, panel_width - 1), axis=0)
    in_panel = (logical_blk < panel_width)[:, None, None]
    panel_factor = jnp.where(in_panel, picked, solved.reshape(row_blocks, BLK, PANEL)).reshape(
        local_rows, PANEL
    )

    ratio = col_count // row_count
    arranged = panel_factor.reshape(col_blocks, ratio, BLK, PANEL)
    chosen = lax.dynamic_index_in_dim(arranged, col_place // row_count, axis=1, keepdims=False)
    chosen = chosen.reshape(col_blocks * BLK, PANEL)
    pairs = []
    for r0 in range(row_count):
        for c1 in range(col_count):
            dest_row = c1 % row_count
            dest_col = r0 + row_count * (c1 // row_count)
            pairs.append((r0 * col_count + c1, dest_row * col_count + dest_col))
    piece_rows = chosen.shape[0] // row_count
    piece = lax.dynamic_slice_in_dim(chosen, (col_place % row_count) * piece_rows, piece_rows, axis=0)
    piece = lax.ppermute(piece, ("row", "col"), pairs)
    copies = jnp.broadcast_to(piece[None], (row_count,) + piece.shape)
    across = lax.all_to_all(copies, "row", split_axis=0, concat_axis=0, tiled=True)
    across = across.reshape(row_count * piece_rows, PANEL)
    update = jnp.einsum("rp,cp->rc", panel_factor, across, precision=exact_mode)
    logical_row = jnp.arange(local_rows) // BLK * row_count + row_place
    logical_col = jnp.arange(local_cols) // BLK * col_count + col_place
    retained = (logical_row >= panel_width)[:, None] & (logical_col >= panel_width)[None, :]
    trailing = jnp.where(retained, extended - update, jnp.zeros_like(update))
    return (trailing, panel_factor)


def solution(mesh):
    in_specs = (P("row", "col"), P(None, "row", "col"), P(), P())
    out_specs = (P("row", "col"), P("row", None))
    return jax.shard_map(
        on_device, mesh=mesh, in_specs=in_specs, out_specs=out_specs, check_vma=False
    )
```

```python
import jax
import jax.numpy as jnp
from jax import lax
from jax.sharding import PartitionSpec as P

CHILD = 8192
PANEL = 512
BLK = 64


exact_mode = lax.Precision.HIGHEST


def take_slabs(source, indices):
    return jnp.take(source, indices, axis=0)


def factor_and_invert(corner, width=128):
    count = corner.shape[0] // width
    sym = (corner + corner.T) / 2
    grid = [[sym[i * width : (i + 1) * width, j * width : (j + 1) * width] for j in range(count)] for i in range(count)]
    eye = jnp.eye(width, dtype=corner.dtype)
    low = [[None] * count for _ in range(count)]
    diag_inv = []
    for p in range(count):
        lpp = lax.linalg.cholesky(grid[p][p], symmetrize_input=False)
        dinv = jax.scipy.linalg.solve_triangular(lpp, eye, lower=True)
        low[p][p] = lpp
        diag_inv.append(dinv)
        for i in range(p + 1, count):
            low[i][p] = jnp.dot(grid[i][p], dinv.T, precision=exact_mode)
        for i in range(p + 1, count):
            for j in range(p + 1, i + 1):
                grid[i][j] = grid[i][j] - jnp.dot(low[i][p], low[j][p].T, precision=exact_mode)
    zero = jnp.zeros((width, width), corner.dtype)
    inv = [[zero] * count for _ in range(count)]
    for j in range(count):
        inv[j][j] = diag_inv[j]
        for i in range(j + 1, count):
            acc = jnp.dot(low[i][j], inv[j][j], precision=exact_mode)
            for k in range(j + 1, i):
                acc = acc + jnp.dot(low[i][k], inv[k][j], precision=exact_mode)
            inv[i][j] = -jnp.dot(diag_inv[i], acc, precision=exact_mode)
    lower = jnp.block([[low[i][j] if j <= i else zero for j in range(count)] for i in range(count)])
    inverse = jnp.block(inv)
    return lower, inverse


def on_device(front_matrix, child_schur, child_index, child_valid):
    row_count = lax.axis_size("row")
    col_count = lax.axis_size("col")
    row_place = lax.axis_index("row")
    col_place = lax.axis_index("col")
    local_rows, local_cols = front_matrix.shape
    row_blocks = local_rows // BLK
    col_blocks = local_cols // BLK
    child_blocks = CHILD // BLK
    child_rowblk = child_schur.shape[1] // BLK
    child_colblk = child_schur.shape[2] // BLK
    per_owner = child_blocks // (row_count * row_count)
    col_multi = max(1, child_blocks // (col_count * col_count))
    row_slots = row_count * per_owner
    col_slots = col_count * col_multi
    validity = child_valid.astype(jnp.float32)
    all_blocks = jnp.arange(child_blocks)
    owner_row = child_index % row_count
    owner_col = child_index % col_count
    sender_row = all_blocks % row_count
    sender_col = all_blocks % col_count
    before = all_blocks[None, :] < all_blocks[:, None]
    earlier_row = (sender_row[:, None] == sender_row[None, :]) & before
    earlier_col = (sender_col[:, None] == sender_col[None, :]) & before
    row_rank = jnp.sum(
        (earlier_row[None] & (owner_row[:, :, None] == owner_row[:, None, :])).astype(jnp.int32),
        axis=2,
    )
    col_rank = jnp.sum(
        (earlier_col[None] & (owner_col[:, :, None] == owner_col[:, None, :])).astype(jnp.int32),
        axis=2,
    )
    row_key = owner_row * per_owner + row_rank
    col_key = owner_col * col_multi + col_rank
    local_arow = row_place + row_count * jnp.arange(child_rowblk)
    mine_rowkey = jnp.take(row_key, local_arow, axis=1)
    row_hit_send = mine_rowkey[:, :, None] == jnp.arange(row_slots)[None, None, :]
    src_row = jnp.sum(
        row_hit_send.astype(jnp.int32) * jnp.arange(child_rowblk)[None, :, None], axis=1
    )
    local_bcol = col_place + col_count * jnp.arange(child_colblk)
    mine_colkey = jnp.take(col_key, local_bcol, axis=1)
    col_hit_send = mine_colkey[:, :, None] == jnp.arange(col_slots)[None, None, :]
    src_col = jnp.sum(
        col_hit_send.astype(jnp.int32) * jnp.arange(child_colblk)[None, :, None], axis=1
    )
    has_col = jnp.sum(col_hit_send.astype(jnp.float32), axis=1)

    front_rowblk = row_place + row_count * jnp.arange(row_blocks)
    match_rows = (child_index[:, None, :] == front_rowblk[None, :, None]).astype(jnp.int32)
    row_slot_of = sender_row[None, :] * per_owner + row_rank
    row_source = jnp.sum(match_rows * row_slot_of[:, None, :], axis=2)
    row_weight = jnp.sum(match_rows.astype(jnp.float32) * validity[:, None, :], axis=2)
    front_colblk = col_place + col_count * jnp.arange(col_blocks)
    match_cols = (child_index[:, None, :] == front_colblk[None, :, None]).astype(jnp.int32)
    col_slot_of = sender_col[None, :] * col_multi + col_rank
    col_source = jnp.sum(match_cols * col_slot_of[:, None, :], axis=2)
    col_weight = jnp.sum(match_cols.astype(jnp.float32) * validity[:, None, :], axis=2)

    blocks = child_schur.reshape(2, child_rowblk, BLK, child_colblk * BLK)
    section_one = []
    for k in range(2):
        outgoing = take_slabs(blocks[k], src_row[k]).reshape(row_slots * BLK, child_colblk * BLK)
        section_one.append(lax.all_to_all(outgoing, "row", split_axis=0, concat_axis=0, tiled=True))

    panel_width = PANEL // BLK
    corner_blk = jnp.arange(panel_width)
    col_hit = (jnp.take(child_index, local_bcol, axis=1)[:, None, :] == corner_blk[None, :, None])
    corner_cpick = jnp.sum(col_hit.astype(jnp.int32) * jnp.arange(child_colblk)[None, None, :], axis=2)
    corner_cw = jnp.sum(
        col_hit.astype(jnp.float32) * jnp.take(validity, local_bcol, axis=1)[:, None, :], axis=2
    )
    own = jnp.where(col_place < panel_width, front_matrix[:BLK, :BLK], jnp.zeros((BLK, BLK), jnp.float32))
    partial = lax.dynamic_update_slice(
        jnp.zeros((BLK, PANEL), jnp.float32), own, (0, jnp.minimum(col_place, panel_width - 1) * BLK)
    )
    for k in range(2):
        slab = lax.dynamic_slice_in_dim(section_one[k], row_source[k, 0] * BLK, BLK, axis=0)
        slab = (slab * row_weight[k, 0]).reshape(BLK, child_colblk, BLK)
        picked_cols = jnp.take(slab, corner_cpick[k], axis=1) * corner_cw[k][None, :, None]
        partial = partial + picked_cols.reshape(BLK, PANEL)
    share = partial.reshape(col_count, BLK // col_count, PANEL)
    share = lax.all_to_all(share, "col", split_axis=0, concat_axis=0, tiled=True)
    share = jnp.sum(share, axis=0)
    spread_share = jnp.broadcast_to(share[None], (col_count,) + share.shape)
    corner_row = lax.all_to_all(spread_share, "col", split_axis=0, concat_axis=0, tiled=True)
    corner_row = corner_row.reshape(BLK, PANEL)
    corner = lax.all_gather(corner_row, "row", axis=0, tiled=True)

    onward = []
    for k in range(2):
        flipped = section_one[k].T.reshape(child_colblk, BLK, row_slots * BLK)
        sent = take_slabs(flipped, src_col[k]) * has_col[k][:, None, None]
        onward.append(sent.reshape(col_slots * BLK, row_slots * BLK))
    onward = jnp.stack(onward)
    lower_factor, inverse = factor_and_invert(corner)
    section_two = lax.all_to_all(onward, "col", split_axis=1, concat_axis=1, tiled=True)
    section_two, lower_factor, inverse = lax.optimization_barrier((section_two, lower_factor, inverse))
    arrived = section_two.reshape(2, col_slots, BLK, row_slots * BLK)

    by_col = jax.vmap(take_slabs)(arrived, col_source) * col_weight[:, :, None, None]
    by_col = by_col.reshape(2, local_cols, row_slots * BLK)
    unflipped = jnp.swapaxes(by_col, 1, 2).reshape(2, row_slots, BLK, local_cols)
    placed = jax.vmap(take_slabs)(unflipped, row_source) * row_weight[:, :, None, None]
    placed = placed.reshape(2, local_rows, local_cols)
    extended = front_matrix + placed[0] + placed[1]

    spread = col_count // panel_width
    lead = front_matrix[:, :BLK]
    for k in range(2):
        first_col = lax.dynamic_index_in_dim(arrived[k], col_source[k, 0], axis=0, keepdims=False)
        first_col = (first_col * col_weight[k, 0]).T.reshape(row_slots, BLK, BLK)
        lead = lead + (take_slabs(first_col, row_source[k]) * row_weight[k][:, None, None]).reshape(
            local_rows, BLK
        )
    part_rows = local_rows // spread
    part = lead[:part_rows]
    for h in range(1, spread):
        moved = lax.ppermute(
            lead[h * part_rows : (h + 1) * part_rows],
            "col",
            [(c, c + panel_width * h) for c in range(panel_width)],
        )
        part = jnp.where(col_place // panel_width == h, moved, part)
    part = part.reshape(part_rows * BLK // 128, 128)
    gathered = lax.all_gather(part, "col", axis=0, tiled=False)
    gathered, extended = lax.optimization_barrier((gathered, extended))
    gathered = gathered.reshape(spread, panel_width, part_rows, BLK)
    panel_cols = gathered.transpose(0, 2, 1, 3).reshape(local_rows, PANEL)

    solved = jnp.einsum("rp,qp->rq", panel_cols, inverse, precision=exact_mode)
    logical_blk = jnp.arange(row_blocks) * row_count + row_place
    factor_blocks = lower_factor.reshape(panel_width, BLK, PANEL)
    picked = jnp.take(factor_blocks, jnp.minimum(logical_blk, panel_width - 1), axis=0)
    in_panel = (logical_blk < panel_width)[:, None, None]
    panel_factor = jnp.where(in_panel, picked, solved.reshape(row_blocks, BLK, PANEL)).reshape(
        local_rows, PANEL
    )

    ratio = col_count // row_count
    arranged = panel_factor.reshape(col_blocks, ratio, BLK, PANEL)
    chosen = lax.dynamic_index_in_dim(arranged, col_place // row_count, axis=1, keepdims=False)
    chosen = chosen.reshape(col_blocks * BLK, PANEL)
    pairs = []
    for r0 in range(row_count):
        for c1 in range(col_count):
            dest_row = c1 % row_count
            dest_col = r0 + row_count * (c1 // row_count)
            pairs.append((r0 * col_count + c1, dest_row * col_count + dest_col))
    piece_rows = chosen.shape[0] // row_count
    piece = lax.dynamic_slice_in_dim(chosen, (col_place % row_count) * piece_rows, piece_rows, axis=0)
    piece = lax.ppermute(piece, ("row", "col"), pairs)
    across = lax.all_gather(piece, "row", axis=0, tiled=True)
    update = jnp.einsum("rp,cp->rc", panel_factor, across, precision=exact_mode)
    logical_row = jnp.arange(local_rows) // BLK * row_count + row_place
    logical_col = jnp.arange(local_cols) // BLK * col_count + col_place
    retained = (logical_row >= panel_width)[:, None] & (logical_col >= panel_width)[None, :]
    trailing = jnp.where(retained, extended - update, jnp.zeros_like(update))
    return (trailing, panel_factor)


def solution(mesh):
    in_specs = (P("row", "col"), P(None, "row", "col"), P(), P())
    out_specs = (P("row", "col"), P("row", None))
    return jax.shard_map(
        on_device, mesh=mesh, in_specs=in_specs, out_specs=out_specs, check_vma=False
    )
```
